1024 devices in a mesh: pipe: 8 (over y, core), seq: 32 (over z), tp: 4 (over x).
Axes of the slice: x: 4, y: 4, z: 32, core: 2. Of those that a mesh axis runs over, the one named last changes fastest.
Arguments:
- upstream: bfloat16 [8, 4, 3072, 2048], P('pipe', 'tp', 'seq'), may hold values from -6 to 6
- queries: bfloat16 [8, 4, 3072, 2048], P('pipe', 'tp', 'seq'), may hold values from -6 to 6
- attention_out: bfloat16 [8, 4, 3072, 2048], P('pipe', 'tp', 'seq'), may hold values from -6 to 6
- keys_values: bfloat16 [8, 4, 32, 3072, 128], P('pipe', 'tp', 'seq'), may hold values from -6 to 6
- log_totals: float32 [8, 4, 32, 3072], P('pipe', 'tp', 'seq'), may hold values from 3.5 to 5.5
- neighbours: int32 [192, 7], replicated, may hold values from -1 to 191, as said below
Outputs:
- query_grad: bfloat16 [8, 4, 32, 3072, 64], P('pipe', 'tp', 'seq')
- cache_grad: bfloat16 [8, 4, 32, 3072, 128], P('pipe', 'tp', 'seq')
The draws below stay inside these ranges and needn't reach their ends.
Inputs may be any that keep to these rules, and one draw needn't show every extreme that they name: `neighbours`: in each row the used entries come first and are distinct; the first is the row's own block; every used entry lies within 4 blocks of the row's block; unused entries are -1. Some aligned run of 48 rows has every row listing as many blocks as lie within reach, up to 7; elsewhere rows list 1 to 3 blocks.
All inputs are finite; a program needn't handle non-finite values.
Results may differ from the reference program's by a relative error of at most 0.0055.
Values may be sent and summed in bfloat16 or wider, within the bound.
No kernel may reach another device: no remote copies, remote signals or barrier semaphores. Data moves between devices by JAX's collectives and lax.ppermute only.
A program may use at most 32 MiB of HBM per device.

```python
import jax
import jax.numpy as jnp
from jax import lax

H = 32
HD = 64
BLK = 64
REACH = 4
NBR = 7
D = 2048
QUART = 3072
QBD = 48
NB = 192
N_PIPE = 8
N_TP = 4


def draw_neighbours(key, part):
    width = 2 * REACH + 1
    key_score, key_count, key_dense = jax.random.split(key, 3)
    offsets = jnp.arange(width, dtype=jnp.int32) - REACH
    rows = jnp.arange(NB, dtype=jnp.int32)
    target = rows[:, None] + offsets[None, :]
    inside = (target >= 0) & (target < NB)
    score = jax.random.randint(key_score, (NB, width), 0, 1 << 20) * width + jnp.arange(width, dtype=jnp.int32)[None, :]
    score = jnp.where(offsets[None, :] == 0, (1 << 20) * width + width, score)
    score = jnp.where(inside, score, -1)
    top_score, order = lax.top_k(score, NBR)
    picked = jnp.take_along_axis(target, order, axis=1)
    reach_count = jnp.sum(inside.astype(jnp.int32), axis=1)
    sparse_count = jax.random.randint(key_count, (NB,), 1, 4)
    dense_quarter = jax.random.randint(key_dense, (), 0, NB // QBD)
    wanted = jnp.where(rows // QBD == dense_quarter, NBR, sparse_count)
    count = jnp.minimum(wanted, reach_count)
    slot = jnp.arange(NBR, dtype=jnp.int32)
    return jnp.where(slot[None, :] < count[:, None], picked, -1).astype(jnp.int32)


def level_of(stream_key, dims, cuts, smallest, top_value):
    gain, own = 1.0, jax.random.fold_in(stream_key, 6)
    for dim, shards_of in cuts:
        heights = jnp.exp(jax.random.uniform(jax.random.fold_in(own, dim), (shards_of,), jnp.float32, smallest / len(cuts), top_value / len(cuts)))
        gain = gain * jnp.repeat(heights, dims[dim] // shards_of).reshape([-1 if axis == dim else 1 for axis in range(len(dims))])
    return gain


def noise(key, dims, spread, limit, shards=(), held_as=jnp.bfloat16):
    factor_of = level_of(key, dims, shards, -0.22, 0.18) if shards else 1.0
    array = jax.random.normal(key, dims, jnp.float32) * spread * factor_of
    return jnp.minimum(jnp.maximum(array, -limit), limit).astype(held_as)


def setup_inputs(seed: int = 0) -> dict:
    arg_keys = jax.random.split(jax.random.key(seed), 7)
    return {
        "upstream": noise(arg_keys[0], (N_PIPE, N_TP, QUART, D), 1.0, 6.0, ((0, 8), (1, 4), (2, 32))),
        "queries": noise(arg_keys[1], (N_PIPE, N_TP, QUART, D), 1.0, 6.0, ((0, 8), (1, 4), (2, 32))),
        "attention_out": noise(arg_keys[2], (N_PIPE, N_TP, QUART, D), 1.0, 6.0, ((0, 8), (1, 4), (2, 32))),
        "keys_values": noise(arg_keys[3], (N_PIPE, N_TP, H, QUART, 2 * HD), 1.0, 6.0, ((0, 8), (1, 4), (2, 32))),
        "log_totals": jnp.clip(3.5 + 2.0 * jax.random.uniform(arg_keys[4], (N_PIPE, N_TP, H, QUART), jnp.float32) ** level_of(arg_keys[4], (N_PIPE, N_TP, H, QUART), ((0, 8), (1, 4), (2, 32)), -0.2, 0.2), 3.5, 5.5),
        "neighbours": draw_neighbours(jax.random.fold_in(arg_keys[6], 71), 0),
    }


def head_grads(query_rows, grad_rows, key_rows, value_rows, norm_rows, delta_rows, neighbours):
    block_total = neighbours.shape[0]
    inv_root = HD ** -0.5
    listed = neighbours >= 0
    key_index = jnp.where(listed, neighbours, 0).astype(jnp.int32)
    query_blocks = query_rows.reshape(block_total, BLK, HD).astype(jnp.float32)
    grad_blocks = grad_rows.reshape(block_total, BLK, HD).astype(jnp.float32)
    key_blocks = key_rows.reshape(block_total, BLK, HD).astype(jnp.float32)
    value_blocks = value_rows.reshape(block_total, BLK, HD).astype(jnp.float32)
    norm_blocks = norm_rows.reshape(block_total, BLK)
    delta_blocks = delta_rows.reshape(block_total, BLK)
    key_taken = key_blocks[key_index]
    value_taken = value_blocks[key_index]
    live_mask = listed.astype(jnp.float32)[:, :, None, None]
    scores = jnp.einsum("aqd,ajkd->ajqk", query_blocks, key_taken) * inv_root
    weights = jnp.exp(scores - norm_blocks[:, None, :, None]) * live_mask
    weights_half = lax.optimization_barrier(weights.astype(jnp.bfloat16)).astype(jnp.float32)
    grad_weights = jnp.einsum("aqd,ajkd->ajqk", grad_blocks, value_taken)
    grad_scores = lax.optimization_barrier((weights * (grad_weights - delta_blocks[:, None, :, None])).astype(jnp.bfloat16)).astype(jnp.float32)
    grad_query = jnp.einsum("ajqk,ajkd->aqd", grad_scores, key_taken) * inv_root
    key_terms = jnp.einsum("ajqk,aqd->ajkd", grad_scores, query_blocks) * inv_root
    value_terms = jnp.einsum("ajqk,aqd->ajkd", weights_half, grad_blocks)
    all_terms = jnp.concatenate([key_terms, value_terms], axis=-1).reshape(-1, BLK, 2 * HD)
    grad_cache = jnp.zeros((block_total, BLK, 2 * HD), jnp.float32).at[key_index.reshape(-1)].add(all_terms)
    return grad_query.reshape(block_total * BLK, HD).astype(jnp.bfloat16), grad_cache.reshape(block_total * BLK, 2 * HD).astype(jnp.bfloat16)


def reference(upstream, queries, attention_out, keys_values, log_totals, neighbours):
    incoming = jnp.roll(upstream, -1, axis=0)
    seq_total = N_TP * QUART

    def section_grads(section_number):
        query_all = queries[section_number].reshape(seq_total, H, HD)
        grad_all = incoming[section_number].reshape(seq_total, H, HD)
        out_all = attention_out[section_number].reshape(seq_total, H, HD)
        row_delta = jnp.sum(grad_all.astype(jnp.float32) * out_all.astype(jnp.float32), axis=2)
        cache_all = jnp.transpose(keys_values[section_number], (1, 0, 2, 3)).reshape(H, seq_total, 2 * HD)
        norm_all = jnp.transpose(log_totals[section_number], (1, 0, 2)).reshape(H, seq_total)

        def one_head(head_number):
            cache_rows = cache_all[head_number]
            return head_grads(query_all[:, head_number, :], grad_all[:, head_number, :], cache_rows[:, :HD], cache_rows[:, HD:], norm_all[head_number], row_delta[:, head_number], neighbours)

        grad_query, grad_cache = lax.map(one_head, jnp.arange(H, dtype=jnp.int32))
        grad_query = jnp.transpose(grad_query.reshape(H, N_TP, QUART, HD), (1, 0, 2, 3))
        grad_cache = jnp.transpose(grad_cache.reshape(H, N_TP, QUART, 2 * HD), (1, 0, 2, 3))
        return grad_query, grad_cache

    query_grad, cache_grad = lax.map(section_grads, jnp.arange(N_PIPE, dtype=jnp.int32))
    return (query_grad, cache_grad)
```

```python
import functools

import jax
import jax.numpy as jnp
from jax import lax
from jax.experimental import pallas as pl
from jax.experimental.pallas import tpu as pltpu
from jax.sharding import PartitionSpec as P

H = 32
HD = 64
BLK = 64
REACH = 4
NBR = 7
WIDTH = 2 * REACH + 1


def passed_along(value, axis, steps):
    count = lax.axis_size(axis)
    pairs = [(source, (source + steps) % count) for source in range(count)]
    return lax.ppermute(value, axis, pairs)


def to_right(value, axis):
    count = lax.axis_size(axis)
    return lax.ppermute(value, axis, [(i, i + 1) for i in range(count - 1)])


def to_left(value, axis):
    count = lax.axis_size(axis)
    return lax.ppermute(value, axis, [(i + 1, i) for i in range(count - 1)])


def band_kernel(mask_ref, q_ref, g_ref, kv_ref, lse_ref, dl_ref, qg_ref, cache_ref):
    blocks = q_ref.shape[0] // BLK
    win = WIDTH * BLK
    cache_ref[...] = jnp.zeros_like(cache_ref)
    row_block = lax.broadcasted_iota(jnp.int32, (win, HD), 0) // BLK

    def step(a, carry):
        r = pl.multiple_of(a * BLK, BLK)
        q = q_ref[pl.ds(r, BLK), :]
        g = g_ref[pl.ds(r, BLK), :]
        kw = kv_ref[pl.ds(r, win), pl.ds(0, HD)]
        vw = kv_ref[pl.ds(r, win), pl.ds(HD, HD)]
        lse = lse_ref[pl.ds(a, 1), :]
        dl = dl_ref[pl.ds(a, 1), :]
        live = jnp.zeros((win, HD), jnp.int32)
        for o in range(WIDTH):
            live = jnp.where(row_block == o, mask_ref[a * WIDTH + o], live)
        nt = (((1,), (1,)), ((), ()))
        st = lax.dot_general(kw, q, nt, preferred_element_type=jnp.float32) * (HD ** -0.5)
        wt = jnp.where(live != 0, jnp.exp(st - lse), 0.0)
        gwt = lax.dot_general(vw, g, nt, preferred_element_type=jnp.float32)
        gst = (wt * (gwt - dl)).astype(jnp.bfloat16)
        wht = wt.astype(jnp.bfloat16)
        tn = (((0,), (0,)), ((), ()))
        qg = lax.dot_general(gst, kw, tn, preferred_element_type=jnp.float32) * (HD ** -0.5)
        qg_ref[pl.ds(r, BLK), :] = qg.astype(qg_ref.dtype)
        kt = jnp.dot(gst, q, preferred_element_type=jnp.float32) * (HD ** -0.5)
        vt = jnp.dot(wht, g, preferred_element_type=jnp.float32)
        cache_ref[pl.ds(r, win), pl.ds(0, HD)] += kt
        cache_ref[pl.ds(r, win), pl.ds(HD, HD)] += vt
        return carry

    lax.fori_loop(0, blocks, step, 0)


def band_grads(mask, q, g, kv_pad, lse, dl):
    rows = q.shape[0]
    blocks = rows // BLK
    pad_rows = kv_pad.shape[0]
    flops = blocks * 5 * 2 * BLK * WIDTH * BLK * HD
    vmem = pl.BlockSpec(memory_space=pltpu.VMEM)
    return pl.pallas_call(
        band_kernel,
        out_shape=(
            jax.ShapeDtypeStruct((rows, HD), jnp.bfloat16),
            jax.ShapeDtypeStruct((pad_rows, 2 * HD), jnp.float32),
        ),
        in_specs=[pl.BlockSpec(memory_space=pltpu.SMEM)] + [vmem] * 5,
        out_specs=(vmem, vmem),
        cost_estimate=pl.CostEstimate(
            flops=flops,
            transcendentals=blocks * WIDTH * BLK * BLK,
            bytes_accessed=rows * HD * 2 * 3 + pad_rows * 2 * HD * 6 + rows * 8,
        ),
    )(mask, q, g, kv_pad, lse, dl)


def body(upstream, queries, attention_out, keys_values, log_totals, neighbours):
    tokens_here = queries.shape[2]
    incoming = passed_along(upstream, "pipe", -1)
    query_tok = queries.reshape(tokens_here, H, HD)
    grad_tok = incoming.reshape(tokens_here, H, HD)
    out_tok = attention_out.reshape(tokens_here, H, HD)
    delta_tok = jnp.sum(grad_tok.astype(jnp.float32) * out_tok.astype(jnp.float32), axis=2)
    query_h = lax.all_to_all(query_tok, "seq", split_axis=1, concat_axis=0, tiled=True)
    grad_h = lax.all_to_all(grad_tok, "seq", split_axis=1, concat_axis=0, tiled=True)
    delta_h = lax.all_to_all(delta_tok, "seq", split_axis=1, concat_axis=0, tiled=True)
    rows_here = query_h.shape[0]
    blocks_here = rows_here // BLK
    query_h = query_h.reshape(rows_here, HD)
    grad_h = grad_h.reshape(rows_here, HD)
    delta_b = delta_h.reshape(blocks_here, BLK)
    lse_b = log_totals.reshape(blocks_here, BLK)
    cache = keys_values.reshape(rows_here, 2 * HD)
    rim = REACH * BLK
    left_halo = to_right(cache[rows_here - rim :], "tp")
    right_halo = to_left(cache[:rim], "tp")
    kv_pad = jnp.concatenate([left_halo, cache, right_halo], axis=0)

    first_block = lax.axis_index("tp") * blocks_here
    listed = lax.dynamic_slice_in_dim(neighbours, first_block, blocks_here, 0)
    own = first_block + jnp.arange(blocks_here, dtype=jnp.int32)
    offset = listed - own[:, None] + REACH
    live = (listed >= 0)[:, :, None] & (offset[:, :, None] == jnp.arange(WIDTH, dtype=jnp.int32)[None, None, :])
    mask = jnp.any(live, axis=1).astype(jnp.int32).reshape(-1)

    query_grad, cache_pad = band_grads(mask, query_h, grad_h, kv_pad, lse_b, delta_b)
    from_right = to_left(cache_pad[:rim], "tp")
    from_left = to_right(cache_pad[rim + rows_here :], "tp")
    own_part = cache_pad[rim : rim + rows_here]
    own_part = jnp.concatenate(
        [
            own_part[:rim] + from_left,
            own_part[rim : rows_here - rim],
            own_part[rows_here - rim :] + from_right,
        ],
        axis=0,
    )
    query_grad = query_grad.reshape(1, 1, 1, rows_here, HD)
    cache_grad = own_part.astype(jnp.bfloat16).reshape(1, 1, 1, rows_here, 2 * HD)
    return (query_grad, cache_grad)


def solution(mesh):
    placed = (
        P("pipe", "tp", "seq", None),
        P("pipe", "tp", "seq", None),
        P("pipe", "tp", "seq", None),
        P("pipe", "tp", "seq", None, None),
        P("pipe", "tp", "seq", None),
        P(),
    )
    return jax.shard_map(
        body,
        mesh=mesh,
        in_specs=placed,
        out_specs=(P("pipe", "tp", "seq", None, None), P("pipe", "tp", "seq", None, None)),
        check_vma=False,
    )
```

```python
import functools

import jax
import jax.numpy as jnp
from jax import lax
from jax.experimental import pallas as pl
from jax.experimental.pallas import tpu as pltpu
from jax.sharding import PartitionSpec as P

H = 32
HD = 64
BLK = 64
REACH = 4
NBR = 7
WIDTH = 2 * REACH + 1


def passed_along(value, axis, steps):
    count = lax.axis_size(axis)
    pairs = [(source, (source + steps) % count) for source in range(count)]
    return lax.ppermute(value, axis, pairs)


def to_right(value, axis):
    count = lax.axis_size(axis)
    return lax.ppermute(value, axis, [(i, i + 1) for i in range(count - 1)])


def to_left(value, axis):
    count = lax.axis_size(axis)
    return lax.ppermute(value, axis, [(i + 1, i) for i in range(count - 1)])


def band_kernel(rz_ref, kv_ref, live_ref, lse_ref, dl_ref, qg_ref, cache_ref):
    steps = rz_ref.shape[0]
    span = 2 * BLK
    win = (WIDTH + 1) * BLK
    cache_ref[...] = jnp.zeros_like(cache_ref)

    def step(i, carry):
        r = pl.multiple_of(i * span, span)
        rz = rz_ref[i]
        kvw = kv_ref[pl.ds(r, win), :]
        nt = (((1,), (1,)), ((), ()))
        both = lax.dot_general(kvw, rz, nt, preferred_element_type=jnp.float32)
        live = jnp.broadcast_to(live_ref[i][:, None, :], (WIDTH + 1, BLK, span)).reshape(win, span)
        lse = lse_ref[pl.ds(i, 1), :]
        dl = dl_ref[pl.ds(i, 1), :]
        wt = jnp.where(live != 0, jnp.exp(both[:, :span] - lse), 0.0)
        gst = (wt * (both[:, span:] - dl)).astype(jnp.bfloat16)
        wht = wt.astype(jnp.bfloat16)
        terms = jnp.dot(
            jnp.concatenate([gst, wht], axis=1), rz, preferred_element_type=jnp.float32
        )
        cache_ref[pl.ds(r, win), :] += terms
        tn = (((0,), (0,)), ((), ()))
        qg = lax.dot_general(gst, kvw, tn, preferred_element_type=jnp.float32)
        qg_ref[pl.ds(r, span), :] = (qg[:, :HD] * (HD ** -0.5)).astype(qg_ref.dtype)
        return carry

    lax.fori_loop(0, steps, step, 0)


def band_grads(rz, kv_pad, live, lse, dl):
    steps = rz.shape[0]
    rows = steps * 2 * BLK
    pad_rows = kv_pad.shape[0]
    win = (WIDTH + 1) * BLK
    flops = steps * 3 * 2 * win * 256 * 128
    vmem = pl.BlockSpec(memory_space=pltpu.VMEM)
    return pl.pallas_call(
        band_kernel,
        out_shape=(
            jax.ShapeDtypeStruct((rows, HD), jnp.bfloat16),
            jax.ShapeDtypeStruct((pad_rows, 2 * HD), jnp.float32),
        ),
        in_specs=[vmem] * 5,
        out_specs=(vmem, vmem),
        cost_estimate=pl.CostEstimate(
            flops=flops,
            transcendentals=steps * win * 128,
            bytes_accessed=rz.size * 2 + pad_rows * 128 * 10 + rows * 10,
        ),
    )(rz, kv_pad, live, lse, dl)


def split3(x):
    hi = lax.reduce_precision(x, exponent_bits=8, mantissa_bits=7)
    rest = x - hi
    mid = lax.reduce_precision(rest, exponent_bits=8, mantissa_bits=7)
    lo = rest - mid
    return jnp.stack([hi, mid, lo], axis=1).astype(jnp.bfloat16)


def local_grads(query_h, grad_h, delta_h, lse_h, kv_pad, listed, first_block):
    rows_here = query_h.shape[0]
    blocks_here = rows_here // BLK
    steps = blocks_here // 2
    lane = 128
    delta_h = delta_h.reshape(steps, 2 * BLK)
    lse_h = lse_h.reshape(steps, 2 * BLK)
    zeros = jnp.zeros((rows_here, HD), jnp.bfloat16)
    top = jnp.concatenate([query_h * jnp.bfloat16(HD ** -0.5), zeros], axis=1)
    bottom = jnp.concatenate([zeros, grad_h], axis=1)
    rz = jnp.concatenate(
        [top.reshape(steps, 2 * BLK, lane), bottom.reshape(steps, 2 * BLK, lane)], axis=1
    )
    own = first_block + jnp.arange(blocks_here, dtype=jnp.int32)
    offset = listed - own[:, None] + REACH
    hit = (listed >= 0)[:, :, None] & (offset[:, :, None] == jnp.arange(WIDTH, dtype=jnp.int32)[None, None, :])
    mask = jnp.any(hit, axis=1).astype(jnp.int32).reshape(steps, 2, WIDTH)
    first_half = jnp.pad(mask[:, 0], ((0, 0), (0, 1)))
    second_half = jnp.pad(mask[:, 1], ((0, 0), (1, 0)))
    live = jnp.concatenate(
        [
            jnp.broadcast_to(first_half[:, :, None], (steps, WIDTH + 1, BLK)),
            jnp.broadcast_to(second_half[:, :, None], (steps, WIDTH + 1, BLK)),
        ],
        axis=2,
    )
    return band_grads(rz, kv_pad, live, lse_h, delta_h)


def body(upstream, queries, attention_out, keys_values, log_totals, neighbours):
    tokens_here = queries.shape[2]
    heads = lax.axis_size("seq")
    incoming = passed_along(upstream, "pipe", -1)
    query_tok = queries.reshape(tokens_here, H, HD)
    grad_tok = incoming.reshape(tokens_here, H, HD)
    out_tok = attention_out.reshape(tokens_here, H, HD)
    delta_tok = jnp.sum(grad_tok.astype(jnp.float32) * out_tok.astype(jnp.float32), axis=2)
    lane = 128
    part_rows = tokens_here * HD // lane
    d_vals = 3 * tokens_here
    d_rows = -(-d_vals // (16 * lane)) * 16
    delta_parts = split3(jnp.transpose(delta_tok)).reshape(H, d_vals)
    delta_parts = jnp.pad(delta_parts, ((0, 0), (0, d_rows * lane - d_vals)))
    send = jnp.concatenate(
        [
            jnp.transpose(query_tok, (1, 0, 2)).reshape(H, part_rows, lane),
            jnp.transpose(grad_tok, (1, 0, 2)).reshape(H, part_rows, lane),
            delta_parts.reshape(H, d_rows, lane),
        ],
        axis=1,
    )
    got = lax.all_to_all(send, "seq", split_axis=0, concat_axis=0, tiled=True)
    rows_here = heads * tokens_here
    blocks_here = rows_here // BLK
    query_h = got[:, :part_rows].reshape(rows_here, HD)
    grad_h = got[:, part_rows : 2 * part_rows].reshape(rows_here, HD)
    d3 = got[:, 2 * part_rows :].reshape(heads, d_rows * lane)[:, :d_vals]
    d3 = d3.reshape(heads, 3, tokens_here).astype(jnp.float32)
    delta_h = ((d3[:, 0] + d3[:, 1]) + d3[:, 2]).reshape(rows_here)
    cache = keys_values.reshape(rows_here, 2 * HD)
    rim = REACH * BLK
    left_halo = to_right(cache[rows_here - rim :], "tp")
    right_halo = to_left(cache[:rim], "tp")
    kv_pad = jnp.concatenate([left_halo, cache, right_halo], axis=0)
    first_block = lax.axis_index("tp") * blocks_here
    listed = lax.dynamic_slice_in_dim(neighbours, first_block, blocks_here, 0)
    query_grad, cache_pad = local_grads(
        query_h, grad_h, delta_h, log_totals.reshape(rows_here), kv_pad, listed, first_block
    )
    from_right = to_left(cache_pad[:rim], "tp")
    from_left = to_right(cache_pad[rim + rows_here :], "tp")
    own_part = cache_pad[rim : rim + rows_here]
    own_part = jnp.concatenate(
        [
            own_part[:rim] + from_left,
            own_part[rim : rows_here - rim],
            own_part[rows_here - rim :] + from_right,
        ],
        axis=0,
    )
    query_grad = query_grad.reshape(1, 1, 1, rows_here, HD)
    cache_grad = own_part.astype(jnp.bfloat16).reshape(1, 1, 1, rows_here, 2 * HD)
    return (query_grad, cache_grad)


def solution(mesh):
    placed = (
        P("pipe", "tp", "seq", None),
        P("pipe", "tp", "seq", None),
        P("pipe", "tp", "seq", None),
        P("pipe", "tp", "seq", None, None),
        P("pipe", "tp", "seq", None),
        P(),
    )
    return jax.shard_map(
        body,
        mesh=mesh,
        in_specs=placed,
        out_specs=(P("pipe", "tp", "seq", None, None), P("pipe", "tp", "seq", None, None)),
        check_vma=False,
    )
```

```python
import functools

import jax
import jax.numpy as jnp
from jax import lax
from jax.experimental import pallas as pl
from jax.experimental.pallas import tpu as pltpu
from jax.sharding import PartitionSpec as P

H = 32
HD = 64
BLK = 64
REACH = 4
NBR = 7
WIDTH = 2 * REACH + 1


def passed_along(value, axis, steps):
    count = lax.axis_size(axis)
    pairs = [(source, (source + steps) % count) for source in range(count)]
    return lax.ppermute(value, axis, pairs)


def to_right(value, axis):
    count = lax.axis_size(axis)
    return lax.ppermute(value, axis, [(i, i + 1) for i in range(count - 1)])


def to_left(value, axis):
    count = lax.axis_size(axis)
    return lax.ppermute(value, axis, [(i + 1, i) for i in range(count - 1)])


def band_kernel(rz_ref, kv_ref, live_ref, lse_ref, dl_ref, qg_ref, cache_ref):
    steps = rz_ref.shape[0]
    span = 2 * BLK
    win = (WIDTH + 1) * BLK
    cache_ref[...] = jnp.zeros_like(cache_ref)

    def step(i, carry):
        r = pl.multiple_of(i * span, span)
        rz = rz_ref[i]
        kvw = kv_ref[pl.ds(r, win), :]
        nt = (((1,), (1,)), ((), ()))
        both = lax.dot_general(kvw, rz, nt, preferred_element_type=jnp.float32)
        live = jnp.broadcast_to(live_ref[i][:, None, :], (WIDTH + 1, BLK, span)).reshape(win, span)
        lse = lse_ref[pl.ds(i, 1), :]
        dl = dl_ref[pl.ds(i, 1), :]
        wt = jnp.where(live != 0, jnp.exp(both[:, :span] - lse), 0.0)
        gst = (wt * (both[:, span:] - dl)).astype(jnp.bfloat16)
        wht = wt.astype(jnp.bfloat16)
        terms = jnp.dot(
            jnp.concatenate([gst, wht], axis=1), rz, preferred_element_type=jnp.float32
        )
        cache_ref[pl.ds(r, win), :] += terms
        tn = (((0,), (0,)), ((), ()))
        qg = lax.dot_general(gst, kvw, tn, preferred_element_type=jnp.float32)
        qg_ref[pl.ds(r, span), :] = (qg[:, :HD] * (HD ** -0.5)).astype(qg_ref.dtype)
        return carry

    lax.fori_loop(0, steps, step, 0, unroll=2)


def band_grads(rz, kv_pad, live, lse, dl):
    steps = rz.shape[0]
    rows = steps * 2 * BLK
    pad_rows = kv_pad.shape[0]
    win = (WIDTH + 1) * BLK
    flops = steps * 3 * 2 * win * 256 * 128
    vmem = pl.BlockSpec(memory_space=pltpu.VMEM)
    return pl.pallas_call(
        band_kernel,
        out_shape=(
            jax.ShapeDtypeStruct((rows, HD), jnp.bfloat16),
            jax.ShapeDtypeStruct((pad_rows, 2 * HD), jnp.float32),
        ),
        in_specs=[vmem] * 5,
        out_specs=(vmem, vmem),
        cost_estimate=pl.CostEstimate(
            flops=flops,
            transcendentals=steps * win * 128,
            bytes_accessed=rz.size * 2 + pad_rows * 128 * 10 + rows * 10,
        ),
    )(rz, kv_pad, live, lse, dl)


def split3(x):
    hi = lax.reduce_precision(x, exponent_bits=8, mantissa_bits=7)
    rest = x - hi
    mid = lax.reduce_precision(rest, exponent_bits=8, mantissa_bits=7)
    lo = rest - mid
    return jnp.stack([hi, mid, lo], axis=1).astype(jnp.bfloat16)


def local_grads(query_h, grad_h, delta_h, lse_h, kv_pad, listed, first_block):
    rows_here = query_h.shape[0]
    blocks_here = rows_here // BLK
    steps = blocks_here // 2
    lane = 128
    delta_h = delta_h.reshape(steps, 2 * BLK)
    lse_h = lse_h.reshape(steps, 2 * BLK)
    zeros = jnp.zeros((rows_here, HD), jnp.bfloat16)
    top = jnp.concatenate([query_h * jnp.bfloat16(HD ** -0.5), zeros], axis=1)
    bottom = jnp.concatenate([zeros, grad_h], axis=1)
    rz = jnp.concatenate(
        [top.reshape(steps, 2 * BLK, lane), bottom.reshape(steps, 2 * BLK, lane)], axis=1
    )
    own = first_block + jnp.arange(blocks_here, dtype=jnp.int32)
    offset = listed - own[:, None] + REACH
    hit = (listed >= 0)[:, :, None] & (offset[:, :, None] == jnp.arange(WIDTH, dtype=jnp.int32)[None, None, :])
    mask = jnp.any(hit, axis=1).astype(jnp.int32).reshape(steps, 2, WIDTH)
    first_half = jnp.pad(mask[:, 0], ((0, 0), (0, 1)))
    second_half = jnp.pad(mask[:, 1], ((0, 0), (1, 0)))
    live = jnp.concatenate(
        [
            jnp.broadcast_to(first_half[:, :, None], (steps, WIDTH + 1, BLK)),
            jnp.broadcast_to(second_half[:, :, None], (steps, WIDTH + 1, BLK)),
        ],
        axis=2,
    )
    return band_grads(rz, kv_pad, live, lse_h, delta_h)


def body(upstream, queries, attention_out, keys_values, log_totals, neighbours):
    tokens_here = queries.shape[2]
    heads = lax.axis_size("seq")
    lane = 128
    part_rows = tokens_here * HD // lane
    query_tok = queries.reshape(tokens_here, H, HD)
    query_send = jnp.transpose(query_tok, (1, 0, 2)).reshape(H, part_rows, lane)
    query_got = lax.all_to_all(query_send, "seq", split_axis=0, concat_axis=0, tiled=True)
    incoming = passed_along(upstream, "pipe", -1)
    grad_tok = incoming.reshape(tokens_here, H, HD)
    out_tok = attention_out.reshape(tokens_here, H, HD)
    delta_tok = jnp.sum(grad_tok.astype(jnp.float32) * out_tok.astype(jnp.float32), axis=2)
    d_vals = 3 * tokens_here
    d_rows = -(-d_vals // (16 * lane)) * 16
    delta_parts = split3(jnp.transpose(delta_tok)).reshape(H, d_vals)
    delta_parts = jnp.pad(delta_parts, ((0, 0), (0, d_rows * lane - d_vals)))
    send = jnp.concatenate(
        [
            jnp.transpose(grad_tok, (1, 0, 2)).reshape(H, part_rows, lane),
            delta_parts.reshape(H, d_rows, lane),
        ],
        axis=1,
    )
    got = lax.all_to_all(send, "seq", split_axis=0, concat_axis=0, tiled=True)
    rows_here = heads * tokens_here
    blocks_here = rows_here // BLK
    query_h = query_got.reshape(rows_here, HD)
    grad_h = got[:, :part_rows].reshape(rows_here, HD)
    d3 = got[:, part_rows:].reshape(heads, d_rows * lane)[:, :d_vals]
    d3 = d3.reshape(heads, 3, tokens_here).astype(jnp.float32)
    delta_h = ((d3[:, 0] + d3[:, 1]) + d3[:, 2]).reshape(rows_here)
    cache = keys_values.reshape(rows_here, 2 * HD)
    rim = REACH * BLK
    left_halo = to_right(cache[rows_here - rim :], "tp")
    right_halo = to_left(cache[:rim], "tp")
    kv_pad = jnp.concatenate([left_halo, cache, right_halo], axis=0)
    first_block = lax.axis_index("tp") * blocks_here
    listed = lax.dynamic_slice_in_dim(neighbours, first_block, blocks_here, 0)
    query_grad, cache_pad = local_grads(
        query_h, grad_h, delta_h, log_totals.reshape(rows_here), kv_pad, listed, first_block
    )
    from_right = to_left(cache_pad[:rim], "tp")
    from_left = to_right(cache_pad[rim + rows_here :], "tp")
    own_part = cache_pad[rim : rim + rows_here]
    own_part = jnp.concatenate(
        [
            own_part[:rim] + from_left,
            own_part[rim : rows_here - rim],
            own_part[rows_here - rim :] + from_right,
        ],
        axis=0,
    )
    query_grad = query_grad.reshape(1, 1, 1, rows_here, HD)
    cache_grad = own_part.astype(jnp.bfloat16).reshape(1, 1, 1, rows_here, 2 * HD)
    return (query_grad, cache_grad)


def solution(mesh):
    placed = (
        P("pipe", "tp", "seq", None),
        P("pipe", "tp", "seq", None),
        P("pipe", "tp", "seq", None),
        P("pipe", "tp", "seq", None, None),
        P("pipe", "tp", "seq", None),
        P(),
    )
    return jax.shard_map(
        body,
        mesh=mesh,
        in_specs=placed,
        out_specs=(P("pipe", "tp", "seq", None, None), P("pipe", "tp", "seq", None, None)),
        check_vma=False,
    )
```

```python
import functools

import jax
import jax.numpy as jnp
from jax import lax
from jax.experimental import pallas as pl
from jax.experimental.pallas import tpu as pltpu
from jax.sharding import PartitionSpec as P

H = 32
HD = 64
BLK = 64
REACH = 4
NBR = 7
WIDTH = 2 * REACH + 1


def passed_along(value, axis, steps):
    count = lax.axis_size(axis)
    pairs = [(source, (source + steps) % count) for source in range(count)]
    return lax.ppermute(value, axis, pairs)


def to_right(value, axis):
    count = lax.axis_size(axis)
    return lax.ppermute(value, axis, [(i, i + 1) for i in range(count - 1)])


def to_left(value, axis):
    count = lax.axis_size(axis)
    return lax.ppermute(value, axis, [(i + 1, i) for i in range(count - 1)])


def band_kernel(rz_ref, kv_ref, live_ref, lse_ref, dl_ref, qg_ref, cache_ref, left_ref, right_ref):
    steps = rz_ref.shape[0]
    span = 2 * BLK
    win = (WIDTH + 1) * BLK
    cache_ref[...] = jnp.zeros_like(cache_ref)

    def step(i, carry):
        r = pl.multiple_of(i * span, span)
        rz = rz_ref[i]
        kvw = kv_ref[pl.ds(r, win), :]
        nt = (((1,), (1,)), ((), ()))
        both = lax.dot_general(kvw, rz, nt, preferred_element_type=jnp.float32)
        live = jnp.broadcast_to(live_ref[i][:, None, :], (WIDTH + 1, BLK, span)).reshape(win, span)
        lse = lse_ref[pl.ds(i, 1), :]
        dl = dl_ref[pl.ds(i, 1), :]
        wt = jnp.where(live != 0, jnp.exp(both[:, :span] - lse), 0.0)
        gst = (wt * (both[:, span:] - dl)).astype(jnp.bfloat16)
        wht = wt.astype(jnp.bfloat16)
        terms = jnp.dot(
            jnp.concatenate([gst, wht], axis=1), rz, preferred_element_type=jnp.float32
        )
        cache_ref[pl.ds(r, win), :] += terms
        tn = (((0,), (0,)), ((), ()))
        qg = lax.dot_general(gst, kvw, tn, preferred_element_type=jnp.float32)
        qg_ref[pl.ds(r, span), :] = (qg[:, :HD] * (HD ** -0.5)).astype(qg_ref.dtype)
        return carry

    lax.fori_loop(0, steps, step, 0, unroll=2)
    rim = REACH * BLK
    left_ref[...] = cache_ref[pl.ds(0, rim), :]
    right_ref[...] = cache_ref[pl.ds(cache_ref.shape[0] - rim, rim), :]


def band_grads(rz, kv_pad, live, lse, dl):
    steps = rz.shape[0]
    rows = steps * 2 * BLK
    pad_rows = kv_pad.shape[0]
    win = (WIDTH + 1) * BLK
    flops = steps * 3 * 2 * win * 256 * 128
    vmem = pl.BlockSpec(memory_space=pltpu.VMEM)
    return pl.pallas_call(
        band_kernel,
        out_shape=(
            jax.ShapeDtypeStruct((rows, HD), jnp.bfloat16),
            jax.ShapeDtypeStruct((pad_rows, 2 * HD), jnp.float32),
            jax.ShapeDtypeStruct((REACH * BLK, 2 * HD), jnp.float32),
            jax.ShapeDtypeStruct((REACH * BLK, 2 * HD), jnp.float32),
        ),
        in_specs=[vmem] * 5,
        out_specs=(vmem, vmem, vmem, vmem),
        cost_estimate=pl.CostEstimate(
            flops=flops,
            transcendentals=steps * win * 128,
            bytes_accessed=rz.size * 2 + pad_rows * 128 * 10 + rows * 10,
        ),
    )(rz, kv_pad, live, lse, dl)


def split3(x):
    hi = lax.reduce_precision(x, exponent_bits=8, mantissa_bits=7)
    rest = x - hi
    mid = lax.reduce_precision(rest, exponent_bits=8, mantissa_bits=7)
    lo = rest - mid
    return jnp.stack([hi, mid, lo], axis=1).astype(jnp.bfloat16)


def local_grads(query_h, grad_h, delta_h, lse_h, kv_pad, listed, first_block):
    rows_here = query_h.shape[0]
    blocks_here = rows_here // BLK
    steps = blocks_here // 2
    lane = 128
    delta_h = delta_h.reshape(steps, 2 * BLK)
    lse_h = lse_h.reshape(steps, 2 * BLK)
    zeros = jnp.zeros((rows_here, HD), jnp.bfloat16)
    top = jnp.concatenate([query_h * jnp.bfloat16(HD ** -0.5), zeros], axis=1)
    bottom = jnp.concatenate([zeros, grad_h], axis=1)
    rz = jnp.concatenate(
        [top.reshape(steps, 2 * BLK, lane), bottom.reshape(steps, 2 * BLK, lane)], axis=1
    )
    own = first_block + jnp.arange(blocks_here, dtype=jnp.int32)
    offset = listed - own[:, None] + REACH
    hit = (listed >= 0)[:, :, None] & (offset[:, :, None] == jnp.arange(WIDTH, dtype=jnp.int32)[None, None, :])
    mask = jnp.any(hit, axis=1).astype(jnp.int32).reshape(steps, 2, WIDTH)
    first_half = jnp.pad(mask[:, 0], ((0, 0), (0, 1)))
    second_half = jnp.pad(mask[:, 1], ((0, 0), (1, 0)))
    live = jnp.concatenate(
        [
            jnp.broadcast_to(first_half[:, :, None], (steps, WIDTH + 1, BLK)),
            jnp.broadcast_to(second_half[:, :, None], (steps, WIDTH + 1, BLK)),
        ],
        axis=2,
    )
    return band_grads(rz, kv_pad, live, lse_h, delta_h)


def body(upstream, queries, attention_out, keys_values, log_totals, neighbours):
    tokens_here = queries.shape[2]
    heads = lax.axis_size("seq")
    incoming = passed_along(upstream, "pipe", -1)
    query_tok = queries.reshape(tokens_here, H, HD)
    grad_tok = incoming.reshape(tokens_here, H, HD)
    out_tok = attention_out.reshape(tokens_here, H, HD)
    delta_tok = jnp.sum(grad_tok.astype(jnp.float32) * out_tok.astype(jnp.float32), axis=2)
    lane = 128
    part_rows = tokens_here * HD // lane
    d_vals = 3 * tokens_here
    d_rows = -(-d_vals // (16 * lane)) * 16
    delta_parts = split3(jnp.transpose(delta_tok)).reshape(H, d_vals)
    delta_parts = jnp.pad(delta_parts, ((0, 0), (0, d_rows * lane - d_vals)))
    send = jnp.concatenate(
        [
            jnp.transpose(query_tok, (1, 0, 2)).reshape(H, part_rows, lane),
            jnp.transpose(grad_tok, (1, 0, 2)).reshape(H, part_rows, lane),
            delta_parts.reshape(H, d_rows, lane),
        ],
        axis=1,
    )
    got = lax.all_to_all(send, "seq", split_axis=0, concat_axis=0, tiled=True)
    rows_here = heads * tokens_here
    blocks_here = rows_here // BLK
    query_h = got[:, :part_rows].reshape(rows_here, HD)
    grad_h = got[:, part_rows : 2 * part_rows].reshape(rows_here, HD)
    d3 = got[:, 2 * part_rows :].reshape(heads, d_rows * lane)[:, :d_vals]
    d3 = d3.reshape(heads, 3, tokens_here).astype(jnp.float32)
    delta_h = ((d3[:, 0] + d3[:, 1]) + d3[:, 2]).reshape(rows_here)
    cache = keys_values.reshape(rows_here, 2 * HD)
    rim = REACH * BLK
    left_halo = to_right(cache[rows_here - rim :], "tp")
    right_halo = to_left(cache[:rim], "tp")
    kv_pad = jnp.concatenate([left_halo, cache, right_halo], axis=0)
    first_block = lax.axis_index("tp") * blocks_here
    listed = lax.dynamic_slice_in_dim(neighbours, first_block, blocks_here, 0)
    query_grad, cache_pad, left_rim, right_rim = local_grads(
        query_h, grad_h, delta_h, log_totals.reshape(rows_here), kv_pad, listed, first_block
    )
    from_right = to_left(left_rim, "tp")
    from_left = to_right(right_rim, "tp")
    own_part = cache_pad[rim : rim + rows_here]
    own_part = jnp.concatenate(
        [
            own_part[:rim] + from_left,
            own_part[rim : rows_here - rim],
            own_part[rows_here - rim :] + from_right,
        ],
        axis=0,
    )
    query_grad = query_grad.reshape(1, 1, 1, rows_here, HD)
    cache_grad = own_part.astype(jnp.bfloat16).reshape(1, 1, 1, rows_here, 2 * HD)
    return (query_grad, cache_grad)


def solution(mesh):
    placed = (
        P("pipe", "tp", "seq", None),
        P("pipe", "tp", "seq", None),
        P("pipe", "tp", "seq", None),
        P("pipe", "tp", "seq", None, None),
        P("pipe", "tp", "seq", None),
        P(),
    )
    return jax.shard_map(
        body,
        mesh=mesh,
        in_specs=placed,
        out_specs=(P("pipe", "tp", "seq", None, None), P("pipe", "tp", "seq", None, None)),
        check_vma=False,
    )
```

```python
import functools

import jax
import jax.numpy as jnp
from jax import lax
from jax.experimental import pallas as pl
from jax.experimental.pallas import tpu as pltpu
from jax.sharding import PartitionSpec as P

H = 32
HD = 64
BLK = 64
REACH = 4
NBR = 7
WIDTH = 2 * REACH + 1


def passed_along(value, axis, steps):
    count = lax.axis_size(axis)
    pairs = [(source, (source + steps) % count) for source in range(count)]
    return lax.ppermute(value, axis, pairs)


def to_right(value, axis):
    count = lax.axis_size(axis)
    return lax.ppermute(value, axis, [(i, i + 1) for i in range(count - 1)])


def to_left(value, axis):
    count = lax.axis_size(axis)
    return lax.ppermute(value, axis, [(i + 1, i) for i in range(count - 1)])


def band_kernel(pair_ref, kv_ref, live_ref, lse_ref, dl_ref, qg_ref, cache_ref, left_ref, right_ref):
    steps = pair_ref.shape[0] // (2 * BLK)
    span = 2 * BLK
    win = (WIDTH + 1) * BLK
    cache_ref[...] = jnp.zeros_like(cache_ref)

    def step(i, carry):
        r = pl.multiple_of(i * span, span)
        pair = pair_ref[pl.ds(r, span), :]
        lane = lax.broadcasted_iota(jnp.int32, pair.shape, 1)
        zero = jnp.zeros_like(pair)
        rz = jnp.concatenate([jnp.where(lane < HD, pair, zero), jnp.where(lane < HD, zero, pair)], axis=0)
        kvw = kv_ref[pl.ds(r, win), :]
        nt = (((1,), (1,)), ((), ()))
        both = lax.dot_general(kvw, rz, nt, preferred_element_type=jnp.float32)
        live = jnp.broadcast_to(live_ref[i][:, None, :], (WIDTH + 1, BLK, span)).reshape(win, span)
        lse = lse_ref[pl.ds(i, 1), :]
        dl = dl_ref[pl.ds(i, 1), :]
        wt = jnp.where(live != 0, jnp.exp(both[:, :span] - lse), 0.0)
        gst = (wt * (both[:, span:] - dl)).astype(jnp.bfloat16)
        wht = wt.astype(jnp.bfloat16)
        terms = jnp.dot(
            jnp.concatenate([gst, wht], axis=1), rz, preferred_element_type=jnp.float32
        )
        cache_ref[pl.ds(r, win), :] += terms
        tn = (((0,), (0,)), ((), ()))
        qg = lax.dot_general(gst, kvw, tn, preferred_element_type=jnp.float32)
        qg_ref[pl.ds(r, span), :] = (qg[:, :HD] * (HD ** -0.5)).astype(qg_ref.dtype)
        return carry

    lax.fori_loop(0, steps, step, 0, unroll=2)
    rim = REACH * BLK
    left_ref[...] = cache_ref[pl.ds(0, rim), :]
    right_ref[...] = cache_ref[pl.ds(cache_ref.shape[0] - rim, rim), :]


def band_grads(pair, kv_pad, live, lse, dl):
    steps = pair.shape[0] // (2 * BLK)
    rows = steps * 2 * BLK
    pad_rows = kv_pad.shape[0]
    win = (WIDTH + 1) * BLK
    flops = steps * 3 * 2 * win * 256 * 128
    vmem = pl.BlockSpec(memory_space=pltpu.VMEM)
    return pl.pallas_call(
        band_kernel,
        out_shape=(
            jax.ShapeDtypeStruct((rows, HD), jnp.bfloat16),
            jax.ShapeDtypeStruct((pad_rows, 2 * HD), jnp.float32),
            jax.ShapeDtypeStruct((REACH * BLK, 2 * HD), jnp.float32),
            jax.ShapeDtypeStruct((REACH * BLK, 2 * HD), jnp.float32),
        ),
        in_specs=[vmem] * 5,
        out_specs=(vmem, vmem, vmem, vmem),
        cost_estimate=pl.CostEstimate(
            flops=flops,
            transcendentals=steps * win * 128,
            bytes_accessed=pair.size * 2 + pad_rows * 128 * 10 + rows * 10,
        ),
    )(pair, kv_pad, live, lse, dl)


def split3(x):
    hi = lax.reduce_precision(x, exponent_bits=8, mantissa_bits=7)
    rest = x - hi
    mid = lax.reduce_precision(rest, exponent_bits=8, mantissa_bits=7)
    lo = rest - mid
    return jnp.stack([hi, mid, lo], axis=1).astype(jnp.bfloat16)


def local_grads(pair, delta_h, lse_h, kv_pad, listed, first_block):
    rows_here = pair.shape[0]
    blocks_here = rows_here // BLK
    steps = blocks_here // 2
    lane = 128
    delta_h = delta_h.reshape(steps, 2 * BLK)
    lse_h = lse_h.reshape(steps, 2 * BLK)
    own = first_block + jnp.arange(blocks_here, dtype=jnp.int32)
    offset = listed - own[:, None] + REACH
    hit = (listed >= 0)[:, :, None] & (offset[:, :, None] == jnp.arange(WIDTH, dtype=jnp.int32)[None, None, :])
    mask = jnp.any(hit, axis=1).astype(jnp.int32).reshape(steps, 2, WIDTH)
    first_half = jnp.pad(mask[:, 0], ((0, 0), (0, 1)))
    second_half = jnp.pad(mask[:, 1], ((0, 0), (1, 0)))
    live = jnp.concatenate(
        [
            jnp.broadcast_to(first_half[:, :, None], (steps, WIDTH + 1, BLK)),
            jnp.broadcast_to(second_half[:, :, None], (steps, WIDTH + 1, BLK)),
        ],
        axis=2,
    )
    return band_grads(pair, kv_pad, live, lse_h, delta_h)


def body(upstream, queries, attention_out, keys_values, log_totals, neighbours):
    tokens_here = queries.shape[2]
    heads = lax.axis_size("seq")
    incoming = passed_along(upstream, "pipe", -1)
    query_tok = queries.reshape(tokens_here, H, HD)
    grad_tok = incoming.reshape(tokens_here, H, HD)
    out_tok = attention_out.reshape(tokens_here, H, HD)
    delta_tok = jnp.sum(grad_tok.astype(jnp.float32) * out_tok.astype(jnp.float32), axis=2)
    lane = 128
    part_rows = tokens_here * HD // lane
    d_vals = 3 * tokens_here
    d_rows = -(-d_vals // (16 * lane)) * 16
    delta_parts = split3(jnp.transpose(delta_tok)).reshape(H, d_vals)
    delta_parts = jnp.pad(delta_parts, ((0, 0), (0, d_rows * lane - d_vals)))
    send = jnp.concatenate(
        [
            jnp.transpose(jnp.concatenate([query_tok * jnp.bfloat16(HD ** -0.5), grad_tok], axis=2), (1, 0, 2)),
            delta_parts.reshape(H, d_rows, lane),
        ],
        axis=1,
    )
    got = lax.all_to_all(send, "seq", split_axis=0, concat_axis=0, tiled=True)
    rows_here = heads * tokens_here
    blocks_here = rows_here // BLK
    pair = got[:, :tokens_here].reshape(rows_here, 2 * HD)
    d3 = got[:, tokens_here:].reshape(heads, d_rows * lane)[:, :d_vals]
    d3 = d3.reshape(heads, 3, tokens_here).astype(jnp.float32)
    delta_h = ((d3[:, 0] + d3[:, 1]) + d3[:, 2]).reshape(rows_here)
    cache = keys_values.reshape(rows_here, 2 * HD)
    rim = REACH * BLK
    left_halo = to_right(cache[rows_here - rim :], "tp")
    right_halo = to_left(cache[:rim], "tp")
    kv_pad = jnp.concatenate([left_halo, cache, right_halo], axis=0)
    first_block = lax.axis_index("tp") * blocks_here
    listed = lax.dynamic_slice_in_dim(neighbours, first_block, blocks_here, 0)
    query_grad, cache_pad, left_rim, right_rim = local_grads(
        pair, delta_h, log_totals.reshape(rows_here), kv_pad, listed, first_block
    )
    from_right = to_left(left_rim, "tp")
    from_left = to_right(right_rim, "tp")
    own_part = cache_pad[rim : rim + rows_here]
    own_part = jnp.concatenate(
        [
            own_part[:rim] + from_left,
            own_part[rim : rows_here - rim],
            own_part[rows_here - rim :] + from_right,
        ],
        axis=0,
    )
    query_grad = query_grad.reshape(1, 1, 1, rows_here, HD)
    cache_grad = own_part.astype(jnp.bfloat16).reshape(1, 1, 1, rows_here, 2 * HD)
    return (query_grad, cache_grad)


def solution(mesh):
    placed = (
        P("pipe", "tp", "seq", None),
        P("pipe", "tp", "seq", None),
        P("pipe", "tp", "seq", None),
        P("pipe", "tp", "seq", None, None),
        P("pipe", "tp", "seq", None),
        P(),
    )
    return jax.shard_map(
        body,
        mesh=mesh,
        in_specs=placed,
        out_specs=(P("pipe", "tp", "seq", None, None), P("pipe", "tp", "seq", None, None)),
        check_vma=False,
    )
```

```python
import functools

import jax
import jax.numpy as jnp
from jax import lax
from jax.experimental import pallas as pl
from jax.experimental.pallas import tpu as pltpu
from jax.sharding import PartitionSpec as P

H = 32
HD = 64
BLK = 64
REACH = 4
NBR = 7
WIDTH = 2 * REACH + 1


def passed_along(value, axis, steps):
    count = lax.axis_size(axis)
    pairs = [(source, (source + steps) % count) for source in range(count)]
    return lax.ppermute(value, axis, pairs)


def to_right(value, axis):
    count = lax.axis_size(axis)
    return lax.ppermute(value, axis, [(i, i + 1) for i in range(count - 1)])


def to_left(value, axis):
    count = lax.axis_size(axis)
    return lax.ppermute(value, axis, [(i + 1, i) for i in range(count - 1)])


def band_kernel(pair_ref, kv_ref, live_ref, lse_ref, dl_ref, qgt_ref, cache_out, ends_ref, rims_ref, cache_ref):
    steps = pair_ref.shape[0] // (2 * BLK)
    span = 2 * BLK
    win = (WIDTH + 1) * BLK
    rim = REACH * BLK
    rows = pair_ref.shape[0]
    cache_ref[...] = jnp.zeros_like(cache_ref)

    def step(i, carry):
        r = pl.multiple_of(i * span, span)
        pair = pair_ref[pl.ds(r, span), :]
        lane = lax.broadcasted_iota(jnp.int32, pair.shape, 1)
        zero = jnp.zeros_like(pair)
        rz = jnp.concatenate([jnp.where(lane < HD, pair, zero), jnp.where(lane < HD, zero, pair)], axis=0)
        kvw = kv_ref[pl.ds(r, win), :]
        nt = (((1,), (1,)), ((), ()))
        both = lax.dot_general(kvw, rz, nt, preferred_element_type=jnp.float32)
        live = jnp.broadcast_to(live_ref[i][:, None, :], (WIDTH + 1, BLK, span)).reshape(win, span)
        lse = lse_ref[pl.ds(i, 1), :]
        dl = dl_ref[pl.ds(i, 1), :]
        wt = jnp.where(live != 0, jnp.exp(both[:, :span] - lse), 0.0)
        gst = (wt * (both[:, span:] - dl)).astype(jnp.bfloat16)
        wht = wt.astype(jnp.bfloat16)
        terms = jnp.dot(
            jnp.concatenate([gst, wht], axis=1), rz, preferred_element_type=jnp.float32
        )
        cache_ref[pl.ds(r, win), :] += terms
        tn = (((0,), (0,)), ((), ()))
        qgt = lax.dot_general(kvw, gst, tn, preferred_element_type=jnp.float32)
        qgt_ref[:, pl.ds(r, span)] = (qgt[:HD] * (HD ** -0.5)).astype(qgt_ref.dtype)
        return carry

    lax.fori_loop(0, steps, step, 0, unroll=2)
    cache_out[...] = cache_ref[pl.ds(rim, rows), :].astype(cache_out.dtype)
    ends_ref[0] = cache_ref[pl.ds(rim, rim), :]
    ends_ref[1] = cache_ref[pl.ds(rows, rim), :]
    rims_ref[0] = cache_ref[pl.ds(0, rim), :]
    rims_ref[1] = cache_ref[pl.ds(rows + rim, rim), :]


def band_grads(pair, kv_pad, live, lse, dl):
    rows = pair.shape[0]
    steps = rows // (2 * BLK)
    pad_rows = kv_pad.shape[0]
    win = (WIDTH + 1) * BLK
    rim = REACH * BLK
    flops = steps * 3 * 2 * win * 256 * 128
    vmem = pl.BlockSpec(memory_space=pltpu.VMEM)
    return pl.pallas_call(
        band_kernel,
        out_shape=(
            jax.ShapeDtypeStruct((HD, rows), jnp.bfloat16),
            jax.ShapeDtypeStruct((rows, 2 * HD), jnp.bfloat16),
            jax.ShapeDtypeStruct((2, rim, 2 * HD), jnp.float32),
            jax.ShapeDtypeStruct((2, rim, 2 * HD), jnp.float32),
        ),
        in_specs=[vmem] * 5,
        out_specs=(vmem, vmem, vmem, vmem),
        scratch_shapes=[pltpu.VMEM((pad_rows, 2 * HD), jnp.float32)],
        cost_estimate=pl.CostEstimate(
            flops=flops,
            transcendentals=steps * win * 128,
            bytes_accessed=pair.size * 2 + pad_rows * 128 * 2 + rows * 8 + rows * 128 * 2 + rows * 64 * 2,
        ),
    )(pair, kv_pad, live, lse, dl)


def split3(x):
    hi = lax.reduce_precision(x, exponent_bits=8, mantissa_bits=7)
    rest = x - hi
    mid = lax.reduce_precision(rest, exponent_bits=8, mantissa_bits=7)
    lo = rest - mid
    return jnp.stack([hi, mid, lo], axis=1).astype(jnp.bfloat16)


def local_grads(pair, delta_h, lse_h, kv_pad, listed, first_block):
    rows_here = pair.shape[0]
    blocks_here = rows_here // BLK
    steps = blocks_here // 2
    lane = 128
    delta_h = delta_h.reshape(steps, 2 * BLK)
    lse_h = lse_h.reshape(steps, 2 * BLK)
    own = first_block + jnp.arange(blocks_here, dtype=jnp.int32)
    offset = listed - own[:, None] + REACH
    hit = (listed >= 0)[:, :, None] & (offset[:, :, None] == jnp.arange(WIDTH, dtype=jnp.int32)[None, None, :])
    mask = jnp.any(hit, axis=1).astype(jnp.int32).reshape(steps, 2, WIDTH)
    first_half = jnp.pad(mask[:, 0], ((0, 0), (0, 1)))
    second_half = jnp.pad(mask[:, 1], ((0, 0), (1, 0)))
    live = jnp.concatenate(
        [
            jnp.broadcast_to(first_half[:, :, None], (steps, WIDTH + 1, BLK)),
            jnp.broadcast_to(second_half[:, :, None], (steps, WIDTH + 1, BLK)),
        ],
        axis=2,
    )
    return band_grads(pair, kv_pad, live, lse_h, delta_h)


def body(upstream, queries, attention_out, keys_values, log_totals, neighbours):
    tokens_here = queries.shape[2]
    heads = lax.axis_size("seq")
    incoming = passed_along(upstream, "pipe", -1)
    query_tok = queries.reshape(tokens_here, H, HD)
    grad_tok = incoming.reshape(tokens_here, H, HD)
    out_tok = attention_out.reshape(tokens_here, H, HD)
    delta_tok = jnp.sum(grad_tok.astype(jnp.float32) * out_tok.astype(jnp.float32), axis=2)
    lane = 128
    part_rows = tokens_here * HD // lane
    d_vals = 3 * tokens_here
    d_rows = -(-d_vals // (16 * lane)) * 16
    delta_parts = split3(jnp.transpose(delta_tok)).reshape(H, d_vals)
    delta_parts = jnp.pad(delta_parts, ((0, 0), (0, d_rows * lane - d_vals)))
    send = jnp.concatenate(
        [
            jnp.transpose(jnp.concatenate([query_tok * jnp.bfloat16(HD ** -0.5), grad_tok], axis=2), (1, 0, 2)),
            delta_parts.reshape(H, d_rows, lane),
        ],
        axis=1,
    )
    got = lax.all_to_all(send, "seq", split_axis=0, concat_axis=0, tiled=True)
    rows_here = heads * tokens_here
    blocks_here = rows_here // BLK
    pair = got[:, :tokens_here].reshape(rows_here, 2 * HD)
    d3 = got[:, tokens_here:].reshape(heads, d_rows * lane)[:, :d_vals]
    d3 = d3.reshape(heads, 3, tokens_here).astype(jnp.float32)
    delta_h = ((d3[:, 0] + d3[:, 1]) + d3[:, 2]).reshape(rows_here)
    cache = keys_values.reshape(rows_here, 2 * HD)
    rim = REACH * BLK
    left_halo = to_right(cache[rows_here - rim :], "tp")
    right_halo = to_left(cache[:rim], "tp")
    kv_pad = jnp.concatenate([left_halo, cache, right_halo], axis=0)
    first_block = lax.axis_index("tp") * blocks_here
    listed = lax.dynamic_slice_in_dim(neighbours, first_block, blocks_here, 0)
    query_grad_t, cache_own, ends, rims = local_grads(
        pair, delta_h, log_totals.reshape(rows_here), kv_pad, listed, first_block
    )
    from_right = to_left(rims[0], "tp")
    from_left = to_right(rims[1], "tp")
    cache_own = cache_own.at[:rim].set((ends[0] + from_left).astype(jnp.bfloat16))
    cache_own = cache_own.at[rows_here - rim :].set((ends[1] + from_right).astype(jnp.bfloat16))
    query_grad = jnp.transpose(query_grad_t).reshape(1, 1, 1, rows_here, HD)
    cache_grad = cache_own.reshape(1, 1, 1, rows_here, 2 * HD)
    return (query_grad, cache_grad)


def solution(mesh):
    placed = (
        P("pipe", "tp", "seq", None),
        P("pipe", "tp", "seq", None),
        P("pipe", "tp", "seq", None),
        P("pipe", "tp", "seq", None, None),
        P("pipe", "tp", "seq", None),
        P(),
    )
    return jax.shard_map(
        body,
        mesh=mesh,
        in_specs=placed,
        out_specs=(P("pipe", "tp", "seq", None, None), P("pipe", "tp", "seq", None, None)),
        check_vma=False,
    )
```

```python
import functools

import jax
import jax.numpy as jnp
from jax import lax
from jax.experimental import pallas as pl
from jax.experimental.pallas import tpu as pltpu
from jax.sharding import PartitionSpec as P

H = 32
HD = 64
BLK = 64
REACH = 4
NBR = 7
WIDTH = 2 * REACH + 1


def passed_along(value, axis, steps):
    count = lax.axis_size(axis)
    pairs = [(source, (source + steps) % count) for source in range(count)]
    return lax.ppermute(value, axis, pairs)


def to_right(value, axis):
    count = lax.axis_size(axis)
    return lax.ppermute(value, axis, [(i, i + 1) for i in range(count - 1)])


def to_left(value, axis):
    count = lax.axis_size(axis)
    return lax.ppermute(value, axis, [(i + 1, i) for i in range(count - 1)])


def band_kernel(pair_ref, kv_ref, live_ref, lse_ref, dl_ref, qgt_ref, cache_out, ends_ref, rims_ref, cache_ref):
    steps = pair_ref.shape[0] // (2 * BLK)
    span = 2 * BLK
    win = (WIDTH + 1) * BLK
    rim = REACH * BLK
    rows = pair_ref.shape[0]
    cache_ref[...] = jnp.zeros_like(cache_ref)

    def step(i, carry):
        r = pl.multiple_of(i * span, span)
        pair = pair_ref[pl.ds(r, span), :]
        lane = lax.broadcasted_iota(jnp.int32, pair.shape, 1)
        zero = jnp.zeros_like(pair)
        rz = jnp.concatenate([jnp.where(lane < HD, pair, zero), jnp.where(lane < HD, zero, pair)], axis=0)
        kvw = kv_ref[pl.ds(r, win), :]
        nt = (((1,), (1,)), ((), ()))
        both = lax.dot_general(kvw, rz, nt, preferred_element_type=jnp.float32)
        live = jnp.broadcast_to(live_ref[i][:, None, :], (WIDTH + 1, BLK, span)).reshape(win, span)
        lse = lse_ref[pl.ds(i, 1), :]
        dl = dl_ref[pl.ds(i, 1), :]
        wt = jnp.where(live != 0, jnp.exp(both[:, :span] - lse), 0.0)
        gst = (wt * (both[:, span:] - dl)).astype(jnp.bfloat16)
        wht = wt.astype(jnp.bfloat16)
        terms = jnp.dot(
            jnp.concatenate([gst, wht], axis=1), rz, preferred_element_type=jnp.float32
        )
        cache_ref[pl.ds(r, win), :] += terms
        tn = (((0,), (0,)), ((), ()))
        qgt = lax.dot_general(kvw, gst, tn, preferred_element_type=jnp.float32)
        qgt_ref[:, pl.ds(r, span)] = (qgt[:HD] * (HD ** -0.5)).astype(qgt_ref.dtype)
        return carry

    lax.fori_loop(0, steps, step, 0, unroll=2)
    cache_out[...] = cache_ref[pl.ds(rim, rows), :].astype(cache_out.dtype)
    ends_ref[0] = cache_ref[pl.ds(rim, rim), :]
    ends_ref[1] = cache_ref[pl.ds(rows, rim), :]
    rims_ref[0] = cache_ref[pl.ds(0, rim), :]
    rims_ref[1] = cache_ref[pl.ds(rows + rim, rim), :]


def band_grads(pair, kv_pad, live, lse, dl):
    rows = pair.shape[0]
    steps = rows // (2 * BLK)
    pad_rows = kv_pad.shape[0]
    win = (WIDTH + 1) * BLK
    rim = REACH * BLK
    flops = steps * 3 * 2 * win * 256 * 128
    vmem = pl.BlockSpec(memory_space=pltpu.VMEM)
    return pl.pallas_call(
        band_kernel,
        out_shape=(
            jax.ShapeDtypeStruct((HD, rows), jnp.bfloat16),
            jax.ShapeDtypeStruct((rows, 2 * HD), jnp.bfloat16),
            jax.ShapeDtypeStruct((2, rim, 2 * HD), jnp.float32),
            jax.ShapeDtypeStruct((2, rim, 2 * HD), jnp.float32),
        ),
        in_specs=[vmem] * 5,
        out_specs=(vmem, vmem, vmem, vmem),
        scratch_shapes=[pltpu.VMEM((pad_rows, 2 * HD), jnp.float32)],
        cost_estimate=pl.CostEstimate(
            flops=flops,
            transcendentals=steps * win * 128,
            bytes_accessed=pair.size * 2 + pad_rows * 128 * 2 + rows * 8 + rows * 128 * 2 + rows * 64 * 2,
        ),
    )(pair, kv_pad, live, lse, dl)


def split3(x):
    hi = lax.reduce_precision(x, exponent_bits=8, mantissa_bits=7)
    rest = x - hi
    mid = lax.reduce_precision(rest, exponent_bits=8, mantissa_bits=7)
    lo = rest - mid
    return jnp.stack([hi, mid, lo], axis=1).astype(jnp.bfloat16)


def local_grads(pair, delta_h, lse_h, kv_pad, listed, first_block):
    rows_here = pair.shape[0]
    blocks_here = rows_here // BLK
    steps = blocks_here // 2
    lane = 128
    delta_h = delta_h.reshape(steps, 2 * BLK)
    lse_h = lse_h.reshape(steps, 2 * BLK)
    own = first_block + jnp.arange(blocks_here, dtype=jnp.int32)
    offset = listed - own[:, None] + REACH
    hit = (listed >= 0)[:, :, None] & (offset[:, :, None] == jnp.arange(WIDTH, dtype=jnp.int32)[None, None, :])
    mask = jnp.any(hit, axis=1).astype(jnp.int32).reshape(steps, 2, WIDTH)
    first_half = jnp.pad(mask[:, 0], ((0, 0), (0, 1)))
    second_half = jnp.pad(mask[:, 1], ((0, 0), (1, 0)))
    live = jnp.concatenate(
        [
            jnp.broadcast_to(first_half[:, :, None], (steps, WIDTH + 1, BLK)),
            jnp.broadcast_to(second_half[:, :, None], (steps, WIDTH + 1, BLK)),
        ],
        axis=2,
    )
    return band_grads(pair, kv_pad, live, lse_h, delta_h)


def body(upstream, queries, attention_out, keys_values, log_totals, neighbours):
    tokens_here = queries.shape[2]
    heads = lax.axis_size("seq")
    incoming = passed_along(upstream, "pipe", -1)
    query_tok = queries.reshape(tokens_here, H, HD)
    grad_tok = incoming.reshape(tokens_here, H, HD)
    out_tok = attention_out.reshape(tokens_here, H, HD)
    delta_tok = jnp.sum(grad_tok.astype(jnp.float32) * out_tok.astype(jnp.float32), axis=2)
    lane = 128
    part_rows = tokens_here * HD // lane
    d_vals = 3 * tokens_here
    d_rows = -(-d_vals // lane)
    delta_parts = split3(jnp.transpose(delta_tok)).reshape(H, d_vals)
    delta_parts = jnp.pad(delta_parts, ((0, 0), (0, d_rows * lane - d_vals)))
    send = jnp.concatenate(
        [
            jnp.transpose(jnp.concatenate([query_tok * jnp.bfloat16(HD ** -0.5), grad_tok], axis=2), (1, 0, 2)).reshape(H, tokens_here * lane),
            delta_parts,
        ],
        axis=1,
    ).reshape(H, 1, (tokens_here + d_rows) * lane)
    got = lax.all_to_all(send, "seq", split_axis=0, concat_axis=0, tiled=True)
    got = got.reshape(heads, tokens_here + d_rows, lane)
    rows_here = heads * tokens_here
    blocks_here = rows_here // BLK
    pair = got[:, :tokens_here].reshape(rows_here, 2 * HD)
    d3 = got[:, tokens_here:].reshape(heads, d_rows * lane)[:, :d_vals]
    d3 = d3.reshape(heads, 3, tokens_here).astype(jnp.float32)
    delta_h = ((d3[:, 0] + d3[:, 1]) + d3[:, 2]).reshape(rows_here)
    cache = keys_values.reshape(rows_here, 2 * HD)
    rim = REACH * BLK
    left_halo = to_right(cache[rows_here - rim :], "tp")
    right_halo = to_left(cache[:rim], "tp")
    kv_pad = jnp.concatenate([left_halo, cache, right_halo], axis=0)
    first_block = lax.axis_index("tp") * blocks_here
    listed = lax.dynamic_slice_in_dim(neighbours, first_block, blocks_here, 0)
    query_grad_t, cache_own, ends, rims = local_grads(
        pair, delta_h, log_totals.reshape(rows_here), kv_pad, listed, first_block
    )
    from_right = to_left(rims[0], "tp")
    from_left = to_right(rims[1], "tp")
    cache_own = cache_own.at[:rim].set((ends[0] + from_left).astype(jnp.bfloat16))
    cache_own = cache_own.at[rows_here - rim :].set((ends[1] + from_right).astype(jnp.bfloat16))
    query_grad = jnp.transpose(query_grad_t).reshape(1, 1, 1, rows_here, HD)
    cache_grad = cache_own.reshape(1, 1, 1, rows_here, 2 * HD)
    return (query_grad, cache_grad)


def solution(mesh):
    placed = (
        P("pipe", "tp", "seq", None),
        P("pipe", "tp", "seq", None),
        P("pipe", "tp", "seq", None),
        P("pipe", "tp", "seq", None, None),
        P("pipe", "tp", "seq", None),
        P(),
    )
    return jax.shard_map(
        body,
        mesh=mesh,
        in_specs=placed,
        out_specs=(P("pipe", "tp", "seq", None, None), P("pipe", "tp", "seq", None, None)),
        check_vma=False,
    )
```

```python
import functools

import jax
import jax.numpy as jnp
from jax import lax
from jax.experimental import pallas as pl
from jax.experimental.pallas import tpu as pltpu
from jax.sharding import PartitionSpec as P

H = 32
HD = 64
BLK = 64
REACH = 4
NBR = 7
WIDTH = 2 * REACH + 1


def passed_along(value, axis, steps):
    count = lax.axis_size(axis)
    pairs = [(source, (source + steps) % count) for source in range(count)]
    return lax.ppermute(value, axis, pairs)


def to_right(value, axis):
    count = lax.axis_size(axis)
    return lax.ppermute(value, axis, [(i, i + 1) for i in range(count - 1)])


def to_left(value, axis):
    count = lax.axis_size(axis)
    return lax.ppermute(value, axis, [(i + 1, i) for i in range(count - 1)])


def band_kernel(pair_ref, kv_ref, bias_ref, dl_ref, qgt_ref, cache_out, head_ref, tail_ref, left_ref, right_ref, cache_ref):
    steps = pair_ref.shape[0] // (2 * BLK)
    span = 2 * BLK
    win = (WIDTH + 1) * BLK
    rim = REACH * BLK
    rows = pair_ref.shape[0]
    cache_ref[...] = jnp.zeros_like(cache_ref)

    def step(i, carry):
        r = pl.multiple_of(i * span, span)
        pair = pair_ref[pl.ds(r, span), :]
        lane = lax.broadcasted_iota(jnp.int32, pair.shape, 1)
        zero = jnp.zeros_like(pair)
        rz = jnp.concatenate([jnp.where(lane < HD, pair, zero), jnp.where(lane < HD, zero, pair)], axis=0)
        kvw = kv_ref[pl.ds(r, win), :]
        nt = (((1,), (1,)), ((), ()))
        both = lax.dot_general(kvw, rz, nt, preferred_element_type=jnp.float32)
        bias = jnp.broadcast_to(bias_ref[i][:, None, :], (WIDTH + 1, BLK, span)).reshape(win, span)
        dl = dl_ref[pl.ds(i, 1), :]
        wt = jnp.exp(both[:, :span] - bias)
        gst = (wt * (both[:, span:] - dl)).astype(jnp.bfloat16)
        wht = wt.astype(jnp.bfloat16)
        terms = jnp.dot(
            jnp.concatenate([gst, wht], axis=1), rz, preferred_element_type=jnp.float32
        )
        cache_ref[pl.ds(r, win), :] += terms
        tn = (((0,), (0,)), ((), ()))
        qgt = lax.dot_general(kvw, gst, tn, preferred_element_type=jnp.float32)
        qgt_ref[:, pl.ds(r, span)] = (qgt[:HD] * (HD ** -0.5)).astype(qgt_ref.dtype)
        return carry

    lax.fori_loop(0, steps, step, 0, unroll=2)
    cache_out[...] = cache_ref[pl.ds(rim, rows), :].astype(cache_out.dtype)
    head_ref[...] = cache_ref[pl.ds(rim, rim), :]
    tail_ref[...] = cache_ref[pl.ds(rows, rim), :]
    left_ref[...] = cache_ref[pl.ds(0, rim), :]
    right_ref[...] = cache_ref[pl.ds(rows + rim, rim), :]


def band_grads(pair, kv_pad, bias, dl):
    rows = pair.shape[0]
    steps = rows // (2 * BLK)
    pad_rows = kv_pad.shape[0]
    win = (WIDTH + 1) * BLK
    rim = REACH * BLK
    flops = steps * 3 * 2 * win * 256 * 128
    vmem = pl.BlockSpec(memory_space=pltpu.VMEM)
    return pl.pallas_call(
        band_kernel,
        out_shape=(
            jax.ShapeDtypeStruct((HD, rows), jnp.bfloat16),
            jax.ShapeDtypeStruct((rows, 2 * HD), jnp.bfloat16),
        ) + (jax.ShapeDtypeStruct((rim, 2 * HD), jnp.float32),) * 4,
        in_specs=[vmem] * 4,
        out_specs=(vmem,) * 6,
        scratch_shapes=[pltpu.VMEM((pad_rows, 2 * HD), jnp.float32)],
        cost_estimate=pl.CostEstimate(
            flops=flops,
            transcendentals=steps * win * 128,
            bytes_accessed=pair.size * 2 + pad_rows * 128 * 2 + rows * 8 + rows * 128 * 2 + rows * 64 * 2,
        ),
    )(pair, kv_pad, bias, dl)


def split3(x):
    hi = lax.reduce_precision(x, exponent_bits=8, mantissa_bits=7)
    rest = x - hi
    mid = lax.reduce_precision(rest, exponent_bits=8, mantissa_bits=7)
    lo = rest - mid
    return jnp.stack([hi, mid, lo], axis=1).astype(jnp.bfloat16)


def local_grads(pair, delta_h, lse_h, kv_pad, listed, first_block):
    rows_here = pair.shape[0]
    blocks_here = rows_here // BLK
    steps = blocks_here // 2
    lane = 128
    delta_h = delta_h.reshape(steps, 2 * BLK)
    lse_h = lse_h.reshape(steps, 2 * BLK)
    own = first_block + jnp.arange(blocks_here, dtype=jnp.int32)
    offset = listed - own[:, None] + REACH
    hit = (listed >= 0)[:, :, None] & (offset[:, :, None] == jnp.arange(WIDTH, dtype=jnp.int32)[None, None, :])
    mask = jnp.any(hit, axis=1).astype(jnp.int32).reshape(steps, 2, WIDTH)
    first_half = jnp.pad(mask[:, 0], ((0, 0), (0, 1)))
    second_half = jnp.pad(mask[:, 1], ((0, 0), (1, 0)))
    live = jnp.concatenate(
        [
            jnp.broadcast_to(first_half[:, :, None], (steps, WIDTH + 1, BLK)),
            jnp.broadcast_to(second_half[:, :, None], (steps, WIDTH + 1, BLK)),
        ],
        axis=2,
    )
    bias = jnp.where(live != 0, lse_h[:, None, :], jnp.inf)
    return band_grads(pair, kv_pad, bias, delta_h)


def body(upstream, queries, attention_out, keys_values, log_totals, neighbours):
    tokens_here = queries.shape[2]
    heads = lax.axis_size("seq")
    incoming = passed_along(upstream, "pipe", -1)
    query_tok = queries.reshape(tokens_here, H, HD)
    grad_tok = incoming.reshape(tokens_here, H, HD)
    out_tok = attention_out.reshape(tokens_here, H, HD)
    delta_tok = jnp.sum(grad_tok.astype(jnp.float32) * out_tok.astype(jnp.float32), axis=2)
    lane = 128
    part_rows = tokens_here * HD // lane
    d_vals = 3 * tokens_here
    d_rows = -(-d_vals // (16 * lane)) * 16
    delta_parts = split3(jnp.transpose(delta_tok)).reshape(H, d_vals)
    delta_parts = jnp.pad(delta_parts, ((0, 0), (0, d_rows * lane - d_vals)))
    send = jnp.concatenate(
        [
            jnp.transpose(jnp.concatenate([query_tok * jnp.bfloat16(HD ** -0.5), grad_tok], axis=2), (1, 0, 2)),
            delta_parts.reshape(H, d_rows, lane),
        ],
        axis=1,
    )
    got = lax.all_to_all(send, "seq", split_axis=0, concat_axis=0, tiled=True)
    rows_here = heads * tokens_here
    blocks_here = rows_here // BLK
    pair = got[:, :tokens_here].reshape(rows_here, 2 * HD)
    d3 = got[:, tokens_here:].reshape(heads, d_rows * lane)[:, :d_vals]
    d3 = d3.reshape(heads, 3, tokens_here).astype(jnp.float32)
    delta_h = ((d3[:, 0] + d3[:, 1]) + d3[:, 2]).reshape(rows_here)
    cache = keys_values.reshape(rows_here, 2 * HD)
    rim = REACH * BLK
    left_halo = to_right(cache[rows_here - rim :], "tp")
    right_halo = to_left(cache[:rim], "tp")
    kv_pad = jnp.concatenate([left_halo, cache, right_halo], axis=0)
    first_block = lax.axis_index("tp") * blocks_here
    listed = lax.dynamic_slice_in_dim(neighbours, first_block, blocks_here, 0)
    query_grad_t, cache_own, head_part, tail_part, left_rim, right_rim = local_grads(
        pair, delta_h, log_totals.reshape(rows_here), kv_pad, listed, first_block
    )
    from_right = to_left(left_rim, "tp")
    from_left = to_right(right_rim, "tp")
    cache_own = jnp.concatenate(
        [
            (head_part + from_left).astype(jnp.bfloat16),
            cache_own[rim : rows_here - rim],
            (tail_part + from_right).astype(jnp.bfloat16),
        ],
        axis=0,
    )
    query_grad = jnp.transpose(query_grad_t).reshape(1, 1, 1, rows_here, HD)
    cache_grad = cache_own.reshape(1, 1, 1, rows_here, 2 * HD)
    return (query_grad, cache_grad)


def solution(mesh):
    placed = (
        P("pipe", "tp", "seq", None),
        P("pipe", "tp", "seq", None),
        P("pipe", "tp", "seq", None),
        P("pipe", "tp", "seq", None, None),
        P("pipe", "tp", "seq", None),
        P(),
    )
    return jax.shard_map(
        body,
        mesh=mesh,
        in_specs=placed,
        out_specs=(P("pipe", "tp", "seq", None, None), P("pipe", "tp", "seq", None, None)),
        check_vma=False,
    )
```

```python
import functools

import jax
import jax.numpy as jnp
from jax import lax
from jax.experimental import pallas as pl
from jax.experimental.pallas import tpu as pltpu
from jax.sharding import PartitionSpec as P

H = 32
HD = 64
BLK = 64
REACH = 4
NBR = 7
WIDTH = 2 * REACH + 1


def passed_along(value, axis, steps):
    count = lax.axis_size(axis)
    pairs = [(source, (source + steps) % count) for source in range(count)]
    return lax.ppermute(value, axis, pairs)


def to_right(value, axis):
    count = lax.axis_size(axis)
    return lax.ppermute(value, axis, [(i, i + 1) for i in range(count - 1)])


def to_left(value, axis):
    count = lax.axis_size(axis)
    return lax.ppermute(value, axis, [(i + 1, i) for i in range(count - 1)])


def band_kernel(pair_ref, kv_ref, bias_ref, dl_ref, qgt_ref, cache_out, head_ref, tail_ref, left_ref, right_ref, cache_ref):
    steps = pair_ref.shape[0] // (2 * BLK)
    span = 2 * BLK
    win = (WIDTH + 1) * BLK
    rim = REACH * BLK
    rows = pair_ref.shape[0]
    cache_ref[...] = jnp.zeros_like(cache_ref)

    def step(i, carry):
        r = pl.multiple_of(i * span, span)
        pair = pair_ref[pl.ds(r, span), :]
        lane = lax.broadcasted_iota(jnp.int32, pair.shape, 1)
        zero = jnp.zeros_like(pair)
        rz = jnp.concatenate([jnp.where(lane < HD, pair, zero), jnp.where(lane < HD, zero, pair)], axis=0)
        kvw = kv_ref[pl.ds(r, win), :]
        nt = (((1,), (1,)), ((), ()))
        both = lax.dot_general(kvw, rz, nt, preferred_element_type=jnp.float32)
        bias = jnp.broadcast_to(bias_ref[i][:, None, :], (WIDTH + 1, BLK, span)).reshape(win, span)
        dl = dl_ref[pl.ds(i, 1), :]
        wt = jnp.exp(both[:, :span] - bias)
        gst = (wt * (both[:, span:] - dl)).astype(jnp.bfloat16)
        wht = wt.astype(jnp.bfloat16)
        terms = jnp.dot(
            jnp.concatenate([gst, wht], axis=1), rz, preferred_element_type=jnp.float32
        )
        cache_ref[pl.ds(r, win), :] += terms
        tn = (((0,), (0,)), ((), ()))
        qgt = lax.dot_general(kvw, gst, tn, preferred_element_type=jnp.float32)
        qgt_ref[:, pl.ds(r, span)] = (qgt[:HD] * (HD ** -0.5)).astype(qgt_ref.dtype)
        return carry

    lax.fori_loop(0, steps, step, 0, unroll=2)
    cache_out[...] = cache_ref[pl.ds(2 * rim, rows - 2 * rim), :].astype(cache_out.dtype)
    head_ref[...] = cache_ref[pl.ds(rim, rim), :]
    tail_ref[...] = cache_ref[pl.ds(rows, rim), :]
    left_ref[...] = cache_ref[pl.ds(0, rim), :]
    right_ref[...] = cache_ref[pl.ds(rows + rim, rim), :]


def band_grads(pair, kv_pad, bias, dl):
    rows = pair.shape[0]
    steps = rows // (2 * BLK)
    pad_rows = kv_pad.shape[0]
    win = (WIDTH + 1) * BLK
    rim = REACH * BLK
    flops = steps * 3 * 2 * win * 256 * 128
    vmem = pl.BlockSpec(memory_space=pltpu.VMEM)
    return pl.pallas_call(
        band_kernel,
        out_shape=(
            jax.ShapeDtypeStruct((HD, rows), jnp.bfloat16),
            jax.ShapeDtypeStruct((rows - 2 * rim, 2 * HD), jnp.bfloat16),
        ) + (jax.ShapeDtypeStruct((rim, 2 * HD), jnp.float32),) * 4,
        in_specs=[vmem] * 4,
        out_specs=(vmem,) * 6,
        scratch_shapes=[pltpu.VMEM((pad_rows, 2 * HD), jnp.float32)],
        cost_estimate=pl.CostEstimate(
            flops=flops,
            transcendentals=steps * win * 128,
            bytes_accessed=pair.size * 2 + pad_rows * 128 * 2 + rows * 8 + rows * 128 * 2 + rows * 64 * 2,
        ),
    )(pair, kv_pad, bias, dl)


def split3(x):
    hi = lax.reduce_precision(x, exponent_bits=8, mantissa_bits=7)
    rest = x - hi
    mid = lax.reduce_precision(rest, exponent_bits=8, mantissa_bits=7)
    lo = rest - mid
    return jnp.stack([hi, mid, lo], axis=1).astype(jnp.bfloat16)


def local_grads(pair, delta_h, lse_h, kv_pad, listed, first_block):
    rows_here = pair.shape[0]
    blocks_here = rows_here // BLK
    steps = blocks_here // 2
    lane = 128
    delta_h = delta_h.reshape(steps, 2 * BLK)
    lse_h = lse_h.reshape(steps, 2 * BLK)
    own = first_block + jnp.arange(blocks_here, dtype=jnp.int32)
    offset = listed - own[:, None] + REACH
    hit = (listed >= 0)[:, :, None] & (offset[:, :, None] == jnp.arange(WIDTH, dtype=jnp.int32)[None, None, :])
    mask = jnp.any(hit, axis=1).astype(jnp.int32).reshape(steps, 2, WIDTH)
    first_half = jnp.pad(mask[:, 0], ((0, 0), (0, 1)))
    second_half = jnp.pad(mask[:, 1], ((0, 0), (1, 0)))
    live = jnp.concatenate(
        [
            jnp.broadcast_to(first_half[:, :, None], (steps, WIDTH + 1, BLK)),
            jnp.broadcast_to(second_half[:, :, None], (steps, WIDTH + 1, BLK)),
        ],
        axis=2,
    )
    bias = jnp.where(live != 0, lse_h[:, None, :], jnp.inf)
    return band_grads(pair, kv_pad, bias, delta_h)


def body(upstream, queries, attention_out, keys_values, log_totals, neighbours):
    tokens_here = queries.shape[2]
    heads = lax.axis_size("seq")
    incoming = passed_along(upstream, "pipe", -1)
    query_tok = queries.reshape(tokens_here, H, HD)
    grad_tok = incoming.reshape(tokens_here, H, HD)
    out_tok = attention_out.reshape(tokens_here, H, HD)
    delta_tok = jnp.sum(grad_tok.astype(jnp.float32) * out_tok.astype(jnp.float32), axis=2)
    lane = 128
    part_rows = tokens_here * HD // lane
    d_vals = 3 * tokens_here
    d_rows = -(-d_vals // (16 * lane)) * 16
    delta_parts = split3(jnp.transpose(delta_tok)).reshape(H, d_vals)
    delta_parts = jnp.pad(delta_parts, ((0, 0), (0, d_rows * lane - d_vals)))
    send = jnp.concatenate(
        [
            jnp.transpose(jnp.concatenate([query_tok * jnp.bfloat16(HD ** -0.5), grad_tok], axis=2), (1, 0, 2)),
            delta_parts.reshape(H, d_rows, lane),
        ],
        axis=1,
    )
    got = lax.all_to_all(send, "seq", split_axis=0, concat_axis=0, tiled=True)
    rows_here = heads * tokens_here
    blocks_here = rows_here // BLK
    pair = got[:, :tokens_here].reshape(rows_here, 2 * HD)
    d3 = got[:, tokens_here:].reshape(heads, d_rows * lane)[:, :d_vals]
    d3 = d3.reshape(heads, 3, tokens_here).astype(jnp.float32)
    delta_h = ((d3[:, 0] + d3[:, 1]) + d3[:, 2]).reshape(rows_here)
    cache = keys_values.reshape(rows_here, 2 * HD)
    rim = REACH * BLK
    left_halo = to_right(cache[rows_here - rim :], "tp")
    right_halo = to_left(cache[:rim], "tp")
    kv_pad = jnp.concatenate([left_halo, cache, right_halo], axis=0)
    first_block = lax.axis_index("tp") * blocks_here
    listed = lax.dynamic_slice_in_dim(neighbours, first_block, blocks_here, 0)
    query_grad_t, cache_own, head_part, tail_part, left_rim, right_rim = local_grads(
        pair, delta_h, log_totals.reshape(rows_here), kv_pad, listed, first_block
    )
    from_right = to_left(left_rim, "tp")
    from_left = to_right(right_rim, "tp")
    cache_own = jnp.concatenate(
        [
            (head_part + from_left).astype(jnp.bfloat16),
            cache_own,
            (tail_part + from_right).astype(jnp.bfloat16),
        ],
        axis=0,
    )
    query_grad = jnp.transpose(query_grad_t).reshape(1, 1, 1, rows_here, HD)
    cache_grad = cache_own.reshape(1, 1, 1, rows_here, 2 * HD)
    return (query_grad, cache_grad)


def solution(mesh):
    placed = (
        P("pipe", "tp", "seq", None),
        P("pipe", "tp", "seq", None),
        P("pipe", "tp", "seq", None),
        P("pipe", "tp", "seq", None, None),
        P("pipe", "tp", "seq", None),
        P(),
    )
    return jax.shard_map(
        body,
        mesh=mesh,
        in_specs=placed,
        out_specs=(P("pipe", "tp", "seq", None, None), P("pipe", "tp", "seq", None, None)),
        check_vma=False,
    )
```

```python
import functools

import jax
import jax.numpy as jnp
from jax import lax
from jax.experimental import pallas as pl
from jax.experimental.pallas import tpu as pltpu
from jax.sharding import PartitionSpec as P

H = 32
HD = 64
BLK = 64
REACH = 4
NBR = 7
WIDTH = 2 * REACH + 1


def passed_along(value, axis, steps):
    count = lax.axis_size(axis)
    pairs = [(source, (source + steps) % count) for source in range(count)]
    return lax.ppermute(value, axis, pairs)


def to_right(value, axis):
    count = lax.axis_size(axis)
    return lax.ppermute(value, axis, [(i, i + 1) for i in range(count - 1)])


def to_left(value, axis):
    count = lax.axis_size(axis)
    return lax.ppermute(value, axis, [(i + 1, i) for i in range(count - 1)])


def band_kernel(pair_ref, kv_ref, bias_ref, dl_ref, qgt_ref, cache_out, head_ref, tail_ref, left_ref, right_ref, cache_ref):
    steps = pair_ref.shape[0] // (2 * BLK)
    span = 2 * BLK
    win = (WIDTH + 1) * BLK
    rim = REACH * BLK
    rows = pair_ref.shape[0]
    cache_ref[...] = jnp.zeros_like(cache_ref)

    def step(i, carry):
        r = pl.multiple_of(i * span, span)
        pair = pair_ref[pl.ds(r, span), :]
        lane = lax.broadcasted_iota(jnp.int32, pair.shape, 1)
        zero = jnp.zeros_like(pair)
        rz = jnp.concatenate([jnp.where(lane < HD, pair, zero), jnp.where(lane < HD, zero, pair)], axis=0)
        kvw = kv_ref[pl.ds(r, win), :]
        nt = (((1,), (1,)), ((), ()))
        both = lax.dot_general(kvw, rz, nt, preferred_element_type=jnp.float32)
        bias = jnp.broadcast_to(bias_ref[i][:, None, :], (WIDTH + 1, BLK, span)).reshape(win, span)
        dl = dl_ref[pl.ds(i, 1), :]
        wt = jnp.exp(both[:, :span] - bias)
        gst = (wt * (both[:, span:] - dl)).astype(jnp.bfloat16)
        wht = wt.astype(jnp.bfloat16)
        terms = jnp.dot(
            jnp.concatenate([gst, wht], axis=1), rz, preferred_element_type=jnp.float32
        )
        cache_ref[pl.ds(r, win), :] += terms
        tn = (((0,), (0,)), ((), ()))
        qgt = lax.dot_general(kvw, gst, tn, preferred_element_type=jnp.float32)
        qgt_ref[:, pl.ds(r, span)] = (qgt[:HD] * (HD ** -0.5)).astype(qgt_ref.dtype)
        return carry

    lax.fori_loop(0, steps, step, 0, unroll=2)
    cache_out[...] = cache_ref[pl.ds(rim, rows), :].astype(cache_out.dtype)
    head_ref[...] = cache_ref[pl.ds(rim, rim), :]
    tail_ref[...] = cache_ref[pl.ds(rows, rim), :]
    left_ref[...] = cache_ref[pl.ds(0, rim), :]
    right_ref[...] = cache_ref[pl.ds(rows + rim, rim), :]


def band_grads(pair, kv_pad, bias, dl):
    rows = pair.shape[0]
    steps = rows // (2 * BLK)
    pad_rows = kv_pad.shape[0]
    win = (WIDTH + 1) * BLK
    rim = REACH * BLK
    flops = steps * 3 * 2 * win * 256 * 128
    vmem = pl.BlockSpec(memory_space=pltpu.VMEM)
    return pl.pallas_call(
        band_kernel,
        out_shape=(
            jax.ShapeDtypeStruct((HD, rows), jnp.bfloat16),
            jax.ShapeDtypeStruct((rows, 2 * HD), jnp.bfloat16),
        ) + (jax.ShapeDtypeStruct((rim, 2 * HD), jnp.float32),) * 4,
        in_specs=[vmem] * 4,
        out_specs=(vmem,) * 6,
        scratch_shapes=[pltpu.VMEM((pad_rows, 2 * HD), jnp.float32)],
        cost_estimate=pl.CostEstimate(
            flops=flops,
            transcendentals=steps * win * 128,
            bytes_accessed=pair.size * 2 + pad_rows * 128 * 2 + rows * 8 + rows * 128 * 2 + rows * 64 * 2,
        ),
    )(pair, kv_pad, bias, dl)


def split3(x):
    hi = lax.reduce_precision(x, exponent_bits=8, mantissa_bits=7)
    rest = x - hi
    mid = lax.reduce_precision(rest, exponent_bits=8, mantissa_bits=7)
    lo = rest - mid
    return jnp.stack([hi, mid, lo], axis=1).astype(jnp.bfloat16)


def local_grads(pair, delta_h, lse_h, kv_pad, listed, first_block):
    rows_here = pair.shape[0]
    blocks_here = rows_here // BLK
    steps = blocks_here // 2
    lane = 128
    delta_h = delta_h.reshape(steps, 2 * BLK)
    lse_h = lse_h.reshape(steps, 2 * BLK)
    own = first_block + jnp.arange(blocks_here, dtype=jnp.int32)
    offset = listed - own[:, None] + REACH
    hit = (listed >= 0)[:, :, None] & (offset[:, :, None] == jnp.arange(WIDTH, dtype=jnp.int32)[None, None, :])
    mask = jnp.any(hit, axis=1).astype(jnp.int32).reshape(steps, 2, WIDTH)
    first_half = jnp.pad(mask[:, 0], ((0, 0), (0, 1)))
    second_half = jnp.pad(mask[:, 1], ((0, 0), (1, 0)))
    live = jnp.concatenate(
        [
            jnp.broadcast_to(first_half[:, :, None], (steps, WIDTH + 1, BLK)),
            jnp.broadcast_to(second_half[:, :, None], (steps, WIDTH + 1, BLK)),
        ],
        axis=2,
    )
    bias = jnp.where(live != 0, lse_h[:, None, :], jnp.inf)
    return band_grads(pair, kv_pad, bias, delta_h)


def body(upstream, queries, attention_out, keys_values, log_totals, neighbours):
    tokens_here = queries.shape[2]
    heads = lax.axis_size("seq")
    pieces = jnp.split(upstream, 4, axis=2)
    incoming = jnp.concatenate([passed_along(piece, "pipe", -1) for piece in pieces], axis=2)
    query_tok = queries.reshape(tokens_here, H, HD)
    grad_tok = incoming.reshape(tokens_here, H, HD)
    out_tok = attention_out.reshape(tokens_here, H, HD)
    delta_tok = jnp.sum(grad_tok.astype(jnp.float32) * out_tok.astype(jnp.float32), axis=2)
    lane = 128
    part_rows = tokens_here * HD // lane
    d_vals = 3 * tokens_here
    d_rows = -(-d_vals // (16 * lane)) * 16
    delta_parts = split3(jnp.transpose(delta_tok)).reshape(H, d_vals)
    delta_parts = jnp.pad(delta_parts, ((0, 0), (0, d_rows * lane - d_vals)))
    send = jnp.concatenate(
        [
            jnp.transpose(jnp.concatenate([query_tok * jnp.bfloat16(HD ** -0.5), grad_tok], axis=2), (1, 0, 2)),
            delta_parts.reshape(H, d_rows, lane),
        ],
        axis=1,
    )
    got = lax.all_to_all(send, "seq", split_axis=0, concat_axis=0, tiled=True)
    rows_here = heads * tokens_here
    blocks_here = rows_here // BLK
    pair = got[:, :tokens_here].reshape(rows_here, 2 * HD)
    d3 = got[:, tokens_here:].reshape(heads, d_rows * lane)[:, :d_vals]
    d3 = d3.reshape(heads, 3, tokens_here).astype(jnp.float32)
    delta_h = ((d3[:, 0] + d3[:, 1]) + d3[:, 2]).reshape(rows_here)
    cache = keys_values.reshape(rows_here, 2 * HD)
    rim = REACH * BLK
    left_halo = to_right(cache[rows_here - rim :], "tp")
    right_halo = to_left(cache[:rim], "tp")
    kv_pad = jnp.concatenate([left_halo, cache, right_halo], axis=0)
    first_block = lax.axis_index("tp") * blocks_here
    listed = lax.dynamic_slice_in_dim(neighbours, first_block, blocks_here, 0)
    query_grad_t, cache_own, head_part, tail_part, left_rim, right_rim = local_grads(
        pair, delta_h, log_totals.reshape(rows_here), kv_pad, listed, first_block
    )
    from_right = to_left(left_rim, "tp")
    from_left = to_right(right_rim, "tp")
    cache_own = jnp.concatenate(
        [
            (head_part + from_left).astype(jnp.bfloat16),
            cache_own[rim : rows_here - rim],
            (tail_part + from_right).astype(jnp.bfloat16),
        ],
        axis=0,
    )
    query_grad = jnp.transpose(query_grad_t).reshape(1, 1, 1, rows_here, HD)
    cache_grad = cache_own.reshape(1, 1, 1, rows_here, 2 * HD)
    return (query_grad, cache_grad)


def solution(mesh):
    placed = (
        P("pipe", "tp", "seq", None),
        P("pipe", "tp", "seq", None),
        P("pipe", "tp", "seq", None),
        P("pipe", "tp", "seq", None, None),
        P("pipe", "tp", "seq", None),
        P(),
    )
    return jax.shard_map(
        body,
        mesh=mesh,
        in_specs=placed,
        out_specs=(P("pipe", "tp", "seq", None, None), P("pipe", "tp", "seq", None, None)),
        check_vma=False,
    )
```

```python
import functools

import jax
import jax.numpy as jnp
from jax import lax
from jax.experimental import pallas as pl
from jax.experimental.pallas import tpu as pltpu
from jax.sharding import PartitionSpec as P

H = 32
HD = 64
BLK = 64
REACH = 4
NBR = 7
WIDTH = 2 * REACH + 1


def passed_along(value, axis, steps):
    count = lax.axis_size(axis)
    pairs = [(source, (source + steps) % count) for source in range(count)]
    return lax.ppermute(value, axis, pairs)


def to_right(value, axis):
    count = lax.axis_size(axis)
    return lax.ppermute(value, axis, [(i, i + 1) for i in range(count - 1)])


def to_left(value, axis):
    count = lax.axis_size(axis)
    return lax.ppermute(value, axis, [(i + 1, i) for i in range(count - 1)])


def band_kernel(pair_ref, kv_ref, bias_ref, dl_ref, qgt_ref, cache_out, head_ref, tail_ref, left_ref, right_ref, cache_ref):
    steps = pair_ref.shape[0] // (2 * BLK)
    span = 2 * BLK
    win = (WIDTH + 1) * BLK
    rim = REACH * BLK
    rows = pair_ref.shape[0]
    cache_ref[...] = jnp.zeros_like(cache_ref)

    def step(i, carry):
        r = pl.multiple_of(i * span, span)
        pair = pair_ref[pl.ds(r, span), :]
        lane = lax.broadcasted_iota(jnp.int32, pair.shape, 1)
        zero = jnp.zeros_like(pair)
        rz = jnp.concatenate([jnp.where(lane < HD, pair, zero), jnp.where(lane < HD, zero, pair)], axis=0)
        kvw = kv_ref[pl.ds(r, win), :]
        nt = (((1,), (1,)), ((), ()))
        both = lax.dot_general(kvw, rz, nt, preferred_element_type=jnp.float32)
        bias = jnp.broadcast_to(bias_ref[i][:, None, :], (WIDTH + 1, BLK, span)).reshape(win, span)
        dl = dl_ref[pl.ds(i, 1), :]
        wt = jnp.exp(both[:, :span] - bias)
        gst = (wt * (both[:, span:] - dl)).astype(jnp.bfloat16)
        wht = wt.astype(jnp.bfloat16)
        terms = jnp.dot(
            jnp.concatenate([gst, wht], axis=1), rz, preferred_element_type=jnp.float32
        )
        cache_ref[pl.ds(r, win), :] += terms
        tn = (((0,), (0,)), ((), ()))
        qgt = lax.dot_general(kvw, gst, tn, preferred_element_type=jnp.float32)
        qgt_ref[:, pl.ds(r, span)] = (qgt[:HD] * (HD ** -0.5)).astype(qgt_ref.dtype)
        return carry

    lax.fori_loop(0, steps, step, 0, unroll=2)
    cache_out[...] = cache_ref[pl.ds(rim, rows), :].astype(cache_out.dtype)
    head_ref[...] = cache_ref[pl.ds(rim, rim), :]
    tail_ref[...] = cache_ref[pl.ds(rows, rim), :]
    left_ref[...] = cache_ref[pl.ds(0, rim), :].astype(left_ref.dtype)
    right_ref[...] = cache_ref[pl.ds(rows + rim, rim), :].astype(right_ref.dtype)


def band_grads(pair, kv_pad, bias, dl):
    rows = pair.shape[0]
    steps = rows // (2 * BLK)
    pad_rows = kv_pad.shape[0]
    win = (WIDTH + 1) * BLK
    rim = REACH * BLK
    flops = steps * 3 * 2 * win * 256 * 128
    vmem = pl.BlockSpec(memory_space=pltpu.VMEM)
    return pl.pallas_call(
        band_kernel,
        out_shape=(
            jax.ShapeDtypeStruct((HD, rows), jnp.bfloat16),
            jax.ShapeDtypeStruct((rows, 2 * HD), jnp.bfloat16),
        ) + (jax.ShapeDtypeStruct((rim, 2 * HD), jnp.float32),) * 2
        + (jax.ShapeDtypeStruct((rim, 2 * HD), jnp.bfloat16),) * 2,
        in_specs=[vmem] * 4,
        out_specs=(vmem,) * 6,
        scratch_shapes=[pltpu.VMEM((pad_rows, 2 * HD), jnp.float32)],
        cost_estimate=pl.CostEstimate(
            flops=flops,
            transcendentals=steps * win * 128,
            bytes_accessed=pair.size * 2 + pad_rows * 128 * 2 + rows * 8 + rows * 128 * 2 + rows * 64 * 2,
        ),
    )(pair, kv_pad, bias, dl)


def split3(x):
    hi = lax.reduce_precision(x, exponent_bits=8, mantissa_bits=7)
    rest = x - hi
    mid = lax.reduce_precision(rest, exponent_bits=8, mantissa_bits=7)
    lo = rest - mid
    return jnp.stack([hi, mid, lo], axis=1).astype(jnp.bfloat16)


def local_grads(pair, delta_h, lse_h, kv_pad, listed, first_block):
    rows_here = pair.shape[0]
    blocks_here = rows_here // BLK
    steps = blocks_here // 2
    lane = 128
    delta_h = delta_h.reshape(steps, 2 * BLK)
    lse_h = lse_h.reshape(steps, 2 * BLK)
    own = first_block + jnp.arange(blocks_here, dtype=jnp.int32)
    offset = listed - own[:, None] + REACH
    hit = (listed >= 0)[:, :, None] & (offset[:, :, None] == jnp.arange(WIDTH, dtype=jnp.int32)[None, None, :])
    mask = jnp.any(hit, axis=1).astype(jnp.int32).reshape(steps, 2, WIDTH)
    first_half = jnp.pad(mask[:, 0], ((0, 0), (0, 1)))
    second_half = jnp.pad(mask[:, 1], ((0, 0), (1, 0)))
    live = jnp.concatenate(
        [
            jnp.broadcast_to(first_half[:, :, None], (steps, WIDTH + 1, BLK)),
            jnp.broadcast_to(second_half[:, :, None], (steps, WIDTH + 1, BLK)),
        ],
        axis=2,
    )
    bias = jnp.where(live != 0, lse_h[:, None, :], jnp.inf)
    return band_grads(pair, kv_pad, bias, delta_h)


def body(upstream, queries, attention_out, keys_values, log_totals, neighbours):
    tokens_here = queries.shape[2]
    heads = lax.axis_size("seq")
    incoming = passed_along(upstream, "pipe", -1)
    query_tok = queries.reshape(tokens_here, H, HD)
    grad_tok = incoming.reshape(tokens_here, H, HD)
    out_tok = attention_out.reshape(tokens_here, H, HD)
    delta_tok = jnp.sum(grad_tok.astype(jnp.float32) * out_tok.astype(jnp.float32), axis=2)
    lane = 128
    part_rows = tokens_here * HD // lane
    d_vals = 3 * tokens_here
    d_rows = -(-d_vals // (16 * lane)) * 16
    delta_parts = split3(jnp.transpose(delta_tok)).reshape(H, d_vals)
    delta_parts = jnp.pad(delta_parts, ((0, 0), (0, d_rows * lane - d_vals)))
    send = jnp.concatenate(
        [
            jnp.transpose(jnp.concatenate([query_tok * jnp.bfloat16(HD ** -0.5), grad_tok], axis=2), (1, 0, 2)),
            delta_parts.reshape(H, d_rows, lane),
        ],
        axis=1,
    )
    got = lax.all_to_all(send, "seq", split_axis=0, concat_axis=0, tiled=True)
    rows_here = heads * tokens_here
    blocks_here = rows_here // BLK
    pair = got[:, :tokens_here].reshape(rows_here, 2 * HD)
    d3 = got[:, tokens_here:].reshape(heads, d_rows * lane)[:, :d_vals]
    d3 = d3.reshape(heads, 3, tokens_here).astype(jnp.float32)
    delta_h = ((d3[:, 0] + d3[:, 1]) + d3[:, 2]).reshape(rows_here)
    cache = keys_values.reshape(rows_here, 2 * HD)
    rim = REACH * BLK
    left_halo = to_right(cache[rows_here - rim :], "tp")
    right_halo = to_left(cache[:rim], "tp")
    kv_pad = jnp.concatenate([left_halo, cache, right_halo], axis=0)
    first_block = lax.axis_index("tp") * blocks_here
    listed = lax.dynamic_slice_in_dim(neighbours, first_block, blocks_here, 0)
    query_grad_t, cache_own, head_part, tail_part, left_rim, right_rim = local_grads(
        pair, delta_h, log_totals.reshape(rows_here), kv_pad, listed, first_block
    )
    from_right = to_left(left_rim, "tp")
    from_left = to_right(right_rim, "tp")
    cache_own = jnp.concatenate(
        [
            (head_part + from_left.astype(jnp.float32)).astype(jnp.bfloat16),
            cache_own[rim : rows_here - rim],
            (tail_part + from_right.astype(jnp.float32)).astype(jnp.bfloat16),
        ],
        axis=0,
    )
    query_grad = jnp.transpose(query_grad_t).reshape(1, 1, 1, rows_here, HD)
    cache_grad = cache_own.reshape(1, 1, 1, rows_here, 2 * HD)
    return (query_grad, cache_grad)


def solution(mesh):
    placed = (
        P("pipe", "tp", "seq", None),
        P("pipe", "tp", "seq", None),
        P("pipe", "tp", "seq", None),
        P("pipe", "tp", "seq", None, None),
        P("pipe", "tp", "seq", None),
        P(),
    )
    return jax.shard_map(
        body,
        mesh=mesh,
        in_specs=placed,
        out_specs=(P("pipe", "tp", "seq", None, None), P("pipe", "tp", "seq", None, None)),
        check_vma=False,
    )
```

```python
import functools

import jax
import jax.numpy as jnp
from jax import lax
from jax.experimental import pallas as pl
from jax.experimental.pallas import tpu as pltpu
from jax.sharding import PartitionSpec as P

H = 32
HD = 64
BLK = 64
REACH = 4
NBR = 7
WIDTH = 2 * REACH + 1


def passed_along(value, axis, steps):
    count = lax.axis_size(axis)
    pairs = [(source, (source + steps) % count) for source in range(count)]
    return lax.ppermute(value, axis, pairs)


def to_right(value, axis):
    count = lax.axis_size(axis)
    return lax.ppermute(value, axis, [(i, i + 1) for i in range(count - 1)])


def to_left(value, axis):
    count = lax.axis_size(axis)
    return lax.ppermute(value, axis, [(i + 1, i) for i in range(count - 1)])


def band_kernel(pair_ref, kv_ref, bias_ref, dl_ref, qgt_ref, cache_out, head_ref, tail_ref, left_ref, right_ref, cache_ref):
    rows = qgt_ref.shape[1]
    chunk = pair_ref.shape[0] // H
    tokens = rows // H
    span = 2 * BLK
    win = (WIDTH + 1) * BLK
    rim = REACH * BLK
    cache_ref[...] = jnp.zeros_like(cache_ref)

    def step(i, pair):
        r = pl.multiple_of(i * span, span)
        lane = lax.broadcasted_iota(jnp.int32, pair.shape, 1)
        zero = jnp.zeros_like(pair)
        rz = jnp.concatenate([jnp.where(lane < HD, pair, zero), jnp.where(lane < HD, zero, pair)], axis=0)
        kvw = kv_ref[pl.ds(r, win), :]
        nt = (((1,), (1,)), ((), ()))
        both = lax.dot_general(kvw, rz, nt, preferred_element_type=jnp.float32)
        bias = jnp.broadcast_to(bias_ref[i][:, None, :], (WIDTH + 1, BLK, span)).reshape(win, span)
        dl = dl_ref[pl.ds(i, 1), :]
        wt = jnp.exp(both[:, :span] - bias)
        gst = (wt * (both[:, span:] - dl)).astype(jnp.bfloat16)
        wht = wt.astype(jnp.bfloat16)
        terms = jnp.dot(
            jnp.concatenate([gst, wht], axis=1), rz, preferred_element_type=jnp.float32
        )
        cache_ref[pl.ds(r, win), :] += terms
        tn = (((0,), (0,)), ((), ()))
        qgt = lax.dot_general(kvw, gst, tn, preferred_element_type=jnp.float32)
        qgt_ref[:, pl.ds(r, span)] = (qgt[:HD] * (HD ** -0.5)).astype(qgt_ref.dtype)

    per = tokens // (span - tokens)
    group = per + 1

    def grouped(g, carry):
        for c in range(per):
            first = c * span
            src0, off0 = divmod(first, tokens)
            take0 = tokens - off0
            base = g * group
            a = pair_ref[pl.ds(pl.multiple_of((base + src0) * chunk + off0, 16), take0), :]
            b = pair_ref[pl.ds(pl.multiple_of((base + src0 + 1) * chunk, 16), span - take0), :]
            step(g * per + c, jnp.concatenate([a, b], axis=0))
        return carry

    lax.fori_loop(0, rows // (span * per), grouped, 0)
    cache_out[...] = cache_ref[pl.ds(rim, rows), :].astype(cache_out.dtype)
    head_ref[...] = cache_ref[pl.ds(rim, rim), :]
    tail_ref[...] = cache_ref[pl.ds(rows, rim), :]
    left_ref[...] = cache_ref[pl.ds(0, rim), :]
    right_ref[...] = cache_ref[pl.ds(rows + rim, rim), :]


def band_grads(pair, kv_pad, bias, dl):
    rows = dl.size
    steps = rows // (2 * BLK)
    pad_rows = kv_pad.shape[0]
    win = (WIDTH + 1) * BLK
    rim = REACH * BLK
    flops = steps * 3 * 2 * win * 256 * 128
    vmem = pl.BlockSpec(memory_space=pltpu.VMEM)
    return pl.pallas_call(
        band_kernel,
        out_shape=(
            jax.ShapeDtypeStruct((HD, rows), jnp.bfloat16),
            jax.ShapeDtypeStruct((rows, 2 * HD), jnp.bfloat16),
        ) + (jax.ShapeDtypeStruct((rim, 2 * HD), jnp.float32),) * 4,
        in_specs=[vmem] * 4,
        out_specs=(vmem,) * 6,
        scratch_shapes=[pltpu.VMEM((pad_rows, 2 * HD), jnp.float32)],
        cost_estimate=pl.CostEstimate(
            flops=flops,
            transcendentals=steps * win * 128,
            bytes_accessed=pair.size * 2 + pad_rows * 128 * 2 + rows * 8 + rows * 128 * 2 + rows * 64 * 2,
        ),
    )(pair, kv_pad, bias, dl)


def split3(x):
    hi = lax.reduce_precision(x, exponent_bits=8, mantissa_bits=7)
    rest = x - hi
    mid = lax.reduce_precision(rest, exponent_bits=8, mantissa_bits=7)
    lo = rest - mid
    return jnp.stack([hi, mid, lo], axis=1).astype(jnp.bfloat16)


def local_grads(pair, delta_h, lse_h, kv_pad, listed, first_block):
    rows_here = delta_h.shape[0]
    blocks_here = rows_here // BLK
    steps = blocks_here // 2
    lane = 128
    delta_h = delta_h.reshape(steps, 2 * BLK)
    lse_h = lse_h.reshape(steps, 2 * BLK)
    own = first_block + jnp.arange(blocks_here, dtype=jnp.int32)
    offset = listed - own[:, None] + REACH
    hit = (listed >= 0)[:, :, None] & (offset[:, :, None] == jnp.arange(WIDTH, dtype=jnp.int32)[None, None, :])
    mask = jnp.any(hit, axis=1).astype(jnp.int32).reshape(steps, 2, WIDTH)
    first_half = jnp.pad(mask[:, 0], ((0, 0), (0, 1)))
    second_half = jnp.pad(mask[:, 1], ((0, 0), (1, 0)))
    live = jnp.concatenate(
        [
            jnp.broadcast_to(first_half[:, :, None], (steps, WIDTH + 1, BLK)),
            jnp.broadcast_to(second_half[:, :, None], (steps, WIDTH + 1, BLK)),
        ],
        axis=2,
    )
    bias = jnp.where(live != 0, lse_h[:, None, :], jnp.inf)
    return band_grads(pair, kv_pad, bias, delta_h)


def body(upstream, queries, attention_out, keys_values, log_totals, neighbours):
    tokens_here = queries.shape[2]
    heads = lax.axis_size("seq")
    incoming = passed_along(upstream, "pipe", -1)
    query_tok = queries.reshape(tokens_here, H, HD)
    grad_tok = incoming.reshape(tokens_here, H, HD)
    out_tok = attention_out.reshape(tokens_here, H, HD)
    delta_tok = jnp.sum(grad_tok.astype(jnp.float32) * out_tok.astype(jnp.float32), axis=2)
    lane = 128
    part_rows = tokens_here * HD // lane
    d_vals = 3 * tokens_here
    d_rows = -(-d_vals // (16 * lane)) * 16
    delta_parts = split3(jnp.transpose(delta_tok)).reshape(H, d_vals)
    delta_parts = jnp.pad(delta_parts, ((0, 0), (0, d_rows * lane - d_vals)))
    send = jnp.concatenate(
        [
            jnp.transpose(jnp.concatenate([query_tok * jnp.bfloat16(HD ** -0.5), grad_tok], axis=2), (1, 0, 2)),
            delta_parts.reshape(H, d_rows, lane),
        ],
        axis=1,
    )
    got = lax.all_to_all(send, "seq", split_axis=0, concat_axis=0, tiled=True)
    rows_here = heads * tokens_here
    blocks_here = rows_here // BLK
    pair = got.reshape(heads * (tokens_here + d_rows), 2 * HD)
    d3 = got[:, tokens_here:].reshape(heads, d_rows * lane)[:, :d_vals]
    d3 = d3.reshape(heads, 3, tokens_here).astype(jnp.float32)
    delta_h = ((d3[:, 0] + d3[:, 1]) + d3[:, 2]).reshape(rows_here)
    cache = keys_values.reshape(rows_here, 2 * HD)
    rim = REACH * BLK
    left_halo = to_right(cache[rows_here - rim :], "tp")
    right_halo = to_left(cache[:rim], "tp")
    kv_pad = jnp.concatenate([left_halo, cache, right_halo], axis=0)
    first_block = lax.axis_index("tp") * blocks_here
    listed = lax.dynamic_slice_in_dim(neighbours, first_block, blocks_here, 0)
    query_grad_t, cache_own, head_part, tail_part, left_rim, right_rim = local_grads(
        pair, delta_h, log_totals.reshape(rows_here), kv_pad, listed, first_block
    )
    from_right = to_left(left_rim, "tp")
    from_left = to_right(right_rim, "tp")
    cache_own = jnp.concatenate(
        [
            (head_part + from_left).astype(jnp.bfloat16),
            cache_own[rim : rows_here - rim],
            (tail_part + from_right).astype(jnp.bfloat16),
        ],
        axis=0,
    )
    query_grad = jnp.transpose(query_grad_t).reshape(1, 1, 1, rows_here, HD)
    cache_grad = cache_own.reshape(1, 1, 1, rows_here, 2 * HD)
    return (query_grad, cache_grad)


def solution(mesh):
    placed = (
        P("pipe", "tp", "seq", None),
        P("pipe", "tp", "seq", None),
        P("pipe", "tp", "seq", None),
        P("pipe", "tp", "seq", None, None),
        P("pipe", "tp", "seq", None),
        P(),
    )
    return jax.shard_map(
        body,
        mesh=mesh,
        in_specs=placed,
        out_specs=(P("pipe", "tp", "seq", None, None), P("pipe", "tp", "seq", None, None)),
        check_vma=False,
    )
```

```python
import functools

import jax
import jax.numpy as jnp
from jax import lax
from jax.experimental import pallas as pl
from jax.experimental.pallas import tpu as pltpu
from jax.sharding import PartitionSpec as P

H = 32
HD = 64
BLK = 64
REACH = 4
NBR = 7
WIDTH = 2 * REACH + 1


def passed_along(value, axis, steps):
    count = lax.axis_size(axis)
    pairs = [(source, (source + steps) % count) for source in range(count)]
    return lax.ppermute(value, axis, pairs)


def to_right(value, axis):
    count = lax.axis_size(axis)
    return lax.ppermute(value, axis, [(i, i + 1) for i in range(count - 1)])


def to_left(value, axis):
    count = lax.axis_size(axis)
    return lax.ppermute(value, axis, [(i + 1, i) for i in range(count - 1)])


def band_kernel(pair_ref, kv_ref, bias_ref, dl_ref, qgt_ref, cache_out, head_ref, tail_ref, left_ref, right_ref, cache_ref):
    rows = qgt_ref.shape[1]
    chunk = pair_ref.shape[0] // H
    tokens = rows // H
    span = 2 * BLK
    win = (WIDTH + 1) * BLK
    rim = REACH * BLK
    cache_ref[...] = jnp.zeros_like(cache_ref)

    def step(i, pair):
        r = pl.multiple_of(i * span, span)
        lane = lax.broadcasted_iota(jnp.int32, pair.shape, 1)
        zero = jnp.zeros_like(pair)
        rz = jnp.concatenate([jnp.where(lane < HD, pair, zero), jnp.where(lane < HD, zero, pair)], axis=0)
        kvw = kv_ref[pl.ds(r, win), :]
        nt = (((1,), (1,)), ((), ()))
        both = lax.dot_general(kvw, rz, nt, preferred_element_type=jnp.float32)
        bias = jnp.broadcast_to(bias_ref[i][:, None, :], (WIDTH + 1, BLK, span)).reshape(win, span)
        dl = dl_ref[pl.ds(i, 1), :]
        wt = jnp.exp(both[:, :span] - bias)
        gst = (wt * (both[:, span:] - dl)).astype(jnp.bfloat16)
        wht = wt.astype(jnp.bfloat16)
        terms = jnp.dot(
            jnp.concatenate([gst, wht], axis=1), rz, preferred_element_type=jnp.float32
        )
        cache_ref[pl.ds(r, win), :] += terms
        tn = (((0,), (0,)), ((), ()))
        qgt = lax.dot_general(kvw, gst, tn, preferred_element_type=jnp.float32)
        qgt_ref[:, pl.ds(r, span)] = (qgt[:HD] * (HD ** -0.5)).astype(qgt_ref.dtype)

    per = tokens // (span - tokens)
    group = per + 1

    def grouped(g, carry):
        for c in range(per):
            first = c * span
            src0, off0 = divmod(first, tokens)
            take0 = tokens - off0
            base = g * group
            a = pair_ref[pl.ds(pl.multiple_of((base + src0) * chunk + off0, 16), take0), :]
            b = pair_ref[pl.ds(pl.multiple_of((base + src0 + 1) * chunk, 16), span - take0), :]
            step(g * per + c, jnp.concatenate([a, b], axis=0))
        return carry

    lax.fori_loop(0, rows // (span * per), grouped, 0, unroll=2)
    cache_out[...] = cache_ref[pl.ds(rim, rows), :].astype(cache_out.dtype)
    head_ref[...] = cache_ref[pl.ds(rim, rim), :]
    tail_ref[...] = cache_ref[pl.ds(rows, rim), :]
    left_ref[...] = cache_ref[pl.ds(0, rim), :]
    right_ref[...] = cache_ref[pl.ds(rows + rim, rim), :]


def band_grads(pair, kv_pad, bias, dl):
    rows = dl.size
    steps = rows // (2 * BLK)
    pad_rows = kv_pad.shape[0]
    win = (WIDTH + 1) * BLK
    rim = REACH * BLK
    flops = steps * 3 * 2 * win * 256 * 128
    vmem = pl.BlockSpec(memory_space=pltpu.VMEM)
    return pl.pallas_call(
        band_kernel,
        out_shape=(
            jax.ShapeDtypeStruct((HD, rows), jnp.bfloat16),
            jax.ShapeDtypeStruct((rows, 2 * HD), jnp.bfloat16),
        ) + (jax.ShapeDtypeStruct((rim, 2 * HD), jnp.float32),) * 4,
        in_specs=[vmem] * 4,
        out_specs=(vmem,) * 6,
        scratch_shapes=[pltpu.VMEM((pad_rows, 2 * HD), jnp.float32)],
        cost_estimate=pl.CostEstimate(
            flops=flops,
            transcendentals=steps * win * 128,
            bytes_accessed=pair.size * 2 + pad_rows * 128 * 2 + rows * 8 + rows * 128 * 2 + rows * 64 * 2,
        ),
    )(pair, kv_pad, bias, dl)


def split3(x):
    hi = lax.reduce_precision(x, exponent_bits=8, mantissa_bits=7)
    rest = x - hi
    mid = lax.reduce_precision(rest, exponent_bits=8, mantissa_bits=7)
    lo = rest - mid
    return jnp.stack([hi, mid, lo], axis=1).astype(jnp.bfloat16)


def local_grads(pair, delta_h, lse_h, kv_pad, listed, first_block):
    rows_here = delta_h.shape[0]
    blocks_here = rows_here // BLK
    steps = blocks_here // 2
    lane = 128
    delta_h = delta_h.reshape(steps, 2 * BLK)
    lse_h = lse_h.reshape(steps, 2 * BLK)
    own = first_block + jnp.arange(blocks_here, dtype=jnp.int32)
    offset = listed - own[:, None] + REACH
    hit = (listed >= 0)[:, :, None] & (offset[:, :, None] == jnp.arange(WIDTH, dtype=jnp.int32)[None, None, :])
    mask = jnp.any(hit, axis=1).astype(jnp.int32).reshape(steps, 2, WIDTH)
    first_half = jnp.pad(mask[:, 0], ((0, 0), (0, 1)))
    second_half = jnp.pad(mask[:, 1], ((0, 0), (1, 0)))
    live = jnp.concatenate(
        [
            jnp.broadcast_to(first_half[:, :, None], (steps, WIDTH + 1, BLK)),
            jnp.broadcast_to(second_half[:, :, None], (steps, WIDTH + 1, BLK)),
        ],
        axis=2,
    )
    bias = jnp.where(live != 0, lse_h[:, None, :], jnp.inf)
    return band_grads(pair, kv_pad, bias, delta_h)


def body(upstream, queries, attention_out, keys_values, log_totals, neighbours):
    tokens_here = queries.shape[2]
    heads = lax.axis_size("seq")
    incoming = passed_along(upstream, "pipe", -1)
    query_tok = queries.reshape(tokens_here, H, HD)
    grad_tok = incoming.reshape(tokens_here, H, HD)
    out_tok = attention_out.reshape(tokens_here, H, HD)
    delta_tok = jnp.sum(grad_tok.astype(jnp.float32) * out_tok.astype(jnp.float32), axis=2)
    lane = 128
    part_rows = tokens_here * HD // lane
    d_vals = 3 * tokens_here
    d_rows = -(-d_vals // (16 * lane)) * 16
    delta_parts = split3(jnp.transpose(delta_tok)).reshape(H, d_vals)
    delta_parts = jnp.pad(delta_parts, ((0, 0), (0, d_rows * lane - d_vals)))
    send = jnp.concatenate(
        [
            jnp.transpose(jnp.concatenate([query_tok * jnp.bfloat16(HD ** -0.5), grad_tok], axis=2), (1, 0, 2)),
            delta_parts.reshape(H, d_rows, lane),
        ],
        axis=1,
    )
    got = lax.all_to_all(send, "seq", split_axis=0, concat_axis=0, tiled=True)
    rows_here = heads * tokens_here
    blocks_here = rows_here // BLK
    pair = got.reshape(heads * (tokens_here + d_rows), 2 * HD)
    d3 = got[:, tokens_here:].reshape(heads, d_rows * lane)[:, :d_vals]
    d3 = d3.reshape(heads, 3, tokens_here).astype(jnp.float32)
    delta_h = ((d3[:, 0] + d3[:, 1]) + d3[:, 2]).reshape(rows_here)
    cache = keys_values.reshape(rows_here, 2 * HD)
    rim = REACH * BLK
    left_halo = to_right(cache[rows_here - rim :], "tp")
    right_halo = to_left(cache[:rim], "tp")
    kv_pad = jnp.concatenate([left_halo, cache, right_halo], axis=0)
    first_block = lax.axis_index("tp") * blocks_here
    listed = lax.dynamic_slice_in_dim(neighbours, first_block, blocks_here, 0)
    query_grad_t, cache_own, head_part, tail_part, left_rim, right_rim = local_grads(
        pair, delta_h, log_totals.reshape(rows_here), kv_pad, listed, first_block
    )
    from_right = to_left(left_rim, "tp")
    from_left = to_right(right_rim, "tp")
    cache_own = jnp.concatenate(
        [
            (head_part + from_left).astype(jnp.bfloat16),
            cache_own[rim : rows_here - rim],
            (tail_part + from_right).astype(jnp.bfloat16),
        ],
        axis=0,
    )
    query_grad = jnp.transpose(query_grad_t).reshape(1, 1, 1, rows_here, HD)
    cache_grad = cache_own.reshape(1, 1, 1, rows_here, 2 * HD)
    return (query_grad, cache_grad)


def solution(mesh):
    placed = (
        P("pipe", "tp", "seq", None),
        P("pipe", "tp", "seq", None),
        P("pipe", "tp", "seq", None),
        P("pipe", "tp", "seq", None, None),
        P("pipe", "tp", "seq", None),
        P(),
    )
    return jax.shard_map(
        body,
        mesh=mesh,
        in_specs=placed,
        out_specs=(P("pipe", "tp", "seq", None, None), P("pipe", "tp", "seq", None, None)),
        check_vma=False,
    )
```
